128 devices in a mesh: row: 4 (over x_lo, core), col: 32 (over y, z, x_hi).
Axes of the slice: x: 4 (x_hi: 2, x_lo: 2; x = x_hi * 2 + x_lo), y: 4, z: 4, core: 2. Of those that a mesh axis runs over, the one named last changes fastest.
Arguments:
- prompt_tokens: bfloat16 [32768, 2048], P('col', 'row'), may hold values from -6 to 6
- decode_tokens: bfloat16 [32, 2048], P('col', 'row'), may hold values from -6 to 6
- norm_gain: float32 [2048], replicated, may hold values from 0.25 to 1.75
- norm_bias: float32 [2048], replicated, may hold values from -3 to 3
- project_weight: float32 [2048, 6144], P(('row', 'col')), may hold values from -0.25 to 0.25
- dense_weight: float32 [2048, 2048], P(('row', 'col')), may hold values from -0.125 to 0.125
- expand_weight: float32 [2048, 8192], P(('row', 'col')), may hold values from -0.125 to 0.125
- reduce_weight: float32 [2048, 8192], P(('row', 'col')), may hold values from -0.0625 to 0.0625
- key_cache: bfloat16 [32, 32, 262144], P('col', 'row'), may hold values from -15 to 15
- value_cache: bfloat16 [32, 32, 262144], P('col', 'row'), may hold values from -12 to 12
- prompt_lengths: int32 [64], P('col'), may hold values from 128 to 512, as said below
- cache_ages: int32 [32], replicated, may hold values from 1 to 4096, as said below
- slot_request: int32 [32], replicated, may hold values from 0 to 31, each once
Outputs:
- prompt_out: bfloat16 [32768, 2048], P('col', 'row')
- decoded: bfloat16 [32, 2048], P('col', 'row')
The draws below stay inside these ranges and needn't reach their ends.
Inputs may be any that keep to these rules, and one draw needn't show every extreme that they name: `prompt_lengths`: tokens of a prompt at or beyond its length are padding; some prompt is full in every draw. `cache_ages`: cached positions 0 to age - 1 of a request are valid and its new token stands at position age; some request has exactly 4096. `slot_request`: a permutation of the requests.
All inputs are finite; a program needn't handle non-finite values.
Results may differ from the reference program's by a relative error of at most 0.012.
The reference program's roundings to bfloat16 on the way count: a program that leaves them out, or rounds other values in their place, can miss the bound.
Values may be sent and summed in bfloat16 or wider, within the bound.
No kernel may reach another device: no remote copies, remote signals or barrier semaphores. Data moves between devices by JAX's collectives and lax.ppermute only.
A program may use at most 192 MiB of HBM per device.

```python
import jax
import jax.numpy as jnp
from jax import lax

D = 2048
H = 32
HD = 64
ROT = 32
FF = 8192
PLEN = 512
CTX = 4096
PROMPTS = 64
SLOTS = 32


def draw_prompt_lengths(key, part):
    lengths = jax.random.randint(jax.random.fold_in(key, 11), (PROMPTS,), max(1, PLEN // 4), PLEN + 1)
    full_index = jax.random.randint(jax.random.fold_in(key, 12), (), 0, PROMPTS)
    lengths = jnp.where(jnp.arange(PROMPTS) == full_index, PLEN, lengths)
    return lengths.astype(jnp.int32)


def draw_cache_ages(key, part):
    first_draw = jax.random.randint(jax.random.fold_in(key, 21), (SLOTS,), 1, CTX + 1)
    second_draw = jax.random.randint(jax.random.fold_in(key, 22), (SLOTS,), 1, CTX + 1)
    ages = jnp.minimum(first_draw, second_draw)
    oldest = jax.random.randint(jax.random.fold_in(key, 23), (), 0, SLOTS)
    ages = jnp.where(jnp.arange(SLOTS) == oldest, CTX, ages)
    return ages.astype(jnp.int32)


def shard_levels(stream_key, dims, split, low, high):
    def one(dim, parts):
        steps = jax.random.uniform(jax.random.fold_in(jax.random.fold_in(stream_key, 6), dim), (parts,), jnp.float32, low / len(split), high / len(split))
        return jnp.repeat(jnp.exp(steps), dims[dim] // parts).reshape((-1,) + (1,) * (len(dims) - dim - 1))

    level = one(*split[0])
    for cut in split[1:]:
        level = level * one(*cut)
    return level


def bell_draw(key, extent, width, limit, split=(), kind=jnp.bfloat16):
    factor_of = shard_levels(key, extent, split, -0.22, 0.18) if split else 1.0
    result = jax.random.normal(key, extent, jnp.float32) * width * factor_of
    return jnp.minimum(jnp.maximum(result, -limit), limit).astype(kind)


def setup_inputs(seed: int = 0) -> dict:
    splits = jax.random.split(jax.random.key(seed), 14)
    prompt_tokens = bell_draw(splits[0], (PROMPTS * PLEN, D), 1.0, 6.0, ((0, 32), (1, 4)))
    decode_tokens = bell_draw(splits[1], (SLOTS, D), 1.0, 6.0, ((0, 32), (1, 4)))
    norm_gain = jnp.clip(1.0 + 0.15 * jax.random.normal(splits[2], (D,), jnp.float32), 0.25, 1.75)
    norm_bias = bell_draw(splits[3], (D,), 0.5, 3.0, (), jnp.float32)
    project_weight = bell_draw(splits[4], (D, 3 * D), (D // 4) ** -0.5, 0.25, ((0, 128),), jnp.float32)
    dense_weight = bell_draw(splits[5], (D, D), D ** -0.5, 0.125, ((0, 128),), jnp.float32)
    expand_weight = bell_draw(splits[6], (D, FF), D ** -0.5, 0.125, ((0, 128),), jnp.float32)
    reduce_weight = bell_draw(splits[7], (D, FF), FF ** -0.5, 0.0625, ((0, 128),), jnp.float32)
    key_cache = bell_draw(splits[8], (SLOTS, H, CTX * HD), 2.5, 15.0, ((0, 32), (1, 4)))
    value_cache = bell_draw(splits[9], (SLOTS, H, CTX * HD), 2.0, 12.0, ((0, 32), (1, 4)))
    prompt_lengths = draw_prompt_lengths(jax.random.fold_in(splits[13], 71), 0)
    cache_ages = draw_cache_ages(jax.random.fold_in(splits[13], 71), 0)
    slot_request = jax.random.permutation(splits[12], SLOTS).astype(jnp.int32)
    return dict(prompt_tokens=prompt_tokens, decode_tokens=decode_tokens, norm_gain=norm_gain, norm_bias=norm_bias, project_weight=project_weight, dense_weight=dense_weight, expand_weight=expand_weight, reduce_weight=reduce_weight, key_cache=key_cache, value_cache=value_cache, prompt_lengths=prompt_lengths, cache_ages=cache_ages, slot_request=slot_request)


NEG = -1e+30

def layer_norm(rows, gain, bias):
    values = rows.astype(jnp.float32)
    centre = lax.optimization_barrier(jnp.mean(values, axis=-1, keepdims=True))
    centred = values - centre
    deviation = lax.optimization_barrier(jnp.mean(centred * centred, axis=-1, keepdims=True))
    return (centred * lax.rsqrt(deviation + 1e-05) * gain + bias).astype(jnp.bfloat16)

def rotary(vectors, position):
    half_width = ROT // 2
    frequency = 10000.0 ** (-2.0 * jnp.arange(half_width).astype(jnp.float32) / ROT)
    angle = position.astype(jnp.float32)[..., None, None] * frequency
    cosine = jnp.cos(angle)
    sine_value = jnp.sin(angle)
    lower_part = vectors[..., :half_width]
    upper_part = vectors[..., half_width:ROT]
    return jnp.concatenate([lower_part * cosine - upper_part * sine_value, upper_part * cosine + lower_part * sine_value, vectors[..., ROT:]], axis=-1)

def prompt_attention(merged_block, length):
    places = jnp.arange(PLEN).astype(jnp.int32)
    queries = rotary(merged_block[:, :, 0], places).astype(jnp.bfloat16)
    keys_rot = rotary(merged_block[:, :, 1], places).astype(jnp.bfloat16)
    values = merged_block[:, :, 2].astype(jnp.bfloat16)
    scores = jnp.einsum('qhd,khd->hqk', queries.astype(jnp.float32), keys_rot.astype(jnp.float32)) * HD ** (-0.5)
    allowed = (places[None, :] <= places[:, None]) & (places[None, :] < length)
    scores = jnp.where(allowed[None], scores, NEG)
    top = lax.optimization_barrier(jnp.max(scores, axis=-1, keepdims=True))
    raised = jnp.exp(scores - top)
    probs = (raised / lax.optimization_barrier(jnp.sum(raised, axis=-1, keepdims=True))).astype(jnp.bfloat16)
    mixed = jnp.einsum('hqk,khd->qhd', probs.astype(jnp.float32), values.astype(jnp.float32))
    return mixed.astype(jnp.bfloat16).reshape(PLEN, H * HD)

def reference(prompt_tokens, decode_tokens, norm_gain, norm_bias, project_weight, dense_weight, expand_weight, reduce_weight, key_cache, value_cache, prompt_lengths, cache_ages, slot_request):
    w_project = project_weight.astype(jnp.bfloat16)
    w_dense = dense_weight.astype(jnp.bfloat16)
    w_expand = expand_weight.astype(jnp.bfloat16)
    w_reduce = reduce_weight.astype(jnp.bfloat16)
    scale = HD ** (-0.5)

    def feed(rows):
        normed = layer_norm(rows, norm_gain, norm_bias)
        merged = jnp.dot(normed, w_project, preferred_element_type=jnp.float32)
        hidden = jax.nn.gelu(jnp.dot(normed, w_expand, preferred_element_type=jnp.float32), approximate=True).astype(jnp.bfloat16)
        return (merged, hidden)

    def finish(rows, mixed, hidden):
        attn_out = jnp.dot(mixed, w_dense.T, preferred_element_type=jnp.float32)
        mlp_out = jnp.dot(hidden, w_reduce.T, preferred_element_type=jnp.float32)
        return (rows.astype(jnp.float32) + attn_out + mlp_out).astype(jnp.bfloat16)
    merged_p, hidden_p = feed(prompt_tokens)
    blocks = merged_p.reshape(PROMPTS, PLEN, H, 3, HD)
    mixed_p = lax.map(lambda pair: prompt_attention(pair[0], pair[1]), (blocks, prompt_lengths))
    mixed_p = mixed_p.reshape(PROMPTS * PLEN, H * HD)
    prompt_out = finish(prompt_tokens, mixed_p, hidden_p)
    merged_d, hidden_d = feed(decode_tokens)
    slot_age = cache_ages[slot_request]
    pieces = merged_d.reshape(SLOTS, H, 3, HD)
    query_d = rotary(pieces[:, :, 0], slot_age).astype(jnp.bfloat16)
    key_d = rotary(pieces[:, :, 1], slot_age).astype(jnp.bfloat16)
    value_d = pieces[:, :, 2].astype(jnp.bfloat16)

    def one_slot(items):
        query, own_key, own_value, request = items
        keys_all = lax.dynamic_index_in_dim(key_cache, request, 0, keepdims=False).reshape(H, CTX, HD)
        values_all = lax.dynamic_index_in_dim(value_cache, request, 0, keepdims=False).reshape(H, CTX, HD)
        age = lax.dynamic_index_in_dim(cache_ages, request, 0, keepdims=False)
        scores = jnp.einsum('hd,htd->ht', query.astype(jnp.float32), keys_all.astype(jnp.float32)) * scale
        places = jnp.arange(CTX).astype(jnp.int32)
        scores = jnp.where(places[None, :] < age, scores, NEG)
        own_score = lax.optimization_barrier(jnp.sum(query.astype(jnp.float32) * own_key.astype(jnp.float32), axis=-1)) * scale
        top = jnp.maximum(lax.optimization_barrier(jnp.max(scores, axis=-1)), own_score)
        raised = jnp.exp(scores - top[:, None])
        own_raised = jnp.exp(own_score - top)
        total = lax.optimization_barrier(jnp.sum(raised, axis=-1)) + own_raised
        probs = (raised / total[:, None]).astype(jnp.bfloat16)
        own_prob = (own_raised / total).astype(jnp.bfloat16)
        mixed = jnp.einsum('ht,htd->hd', probs.astype(jnp.float32), values_all.astype(jnp.float32))
        mixed = mixed + own_prob.astype(jnp.float32)[:, None] * own_value.astype(jnp.float32)
        return mixed.astype(jnp.bfloat16).reshape(H * HD)
    mixed_d = lax.map(one_slot, (query_d, key_d, value_d, slot_request))
    decoded = finish(decode_tokens, mixed_d, hidden_d)
    return (prompt_out, decoded)
```

```python
import jax
import jax.numpy as jnp
from jax import lax
from jax.sharding import PartitionSpec as P

HD = 64
ROT = 32
PLEN = 512
CTX = 4096
KEY_BLOCK = 512


NEG = -1e30


def layer_norm(rows, gain, bias):
    values = rows.astype(jnp.float32)
    centre = jnp.mean(values, axis=-1, keepdims=True)
    centred = values - centre
    deviation = jnp.mean(centred * centred, axis=-1, keepdims=True)
    return (centred * lax.rsqrt(deviation + 1e-05) * gain + bias).astype(jnp.bfloat16)


def rotary(vectors, position):
    half_width = ROT // 2
    frequency = 10000.0 ** (-2.0 * jnp.arange(half_width).astype(jnp.float32) / ROT)
    angle = position.astype(jnp.float32)[..., None, None] * frequency
    cosine = jnp.cos(angle)
    sine_value = jnp.sin(angle)
    lower_part = vectors[..., :half_width]
    upper_part = vectors[..., half_width:ROT]
    return jnp.concatenate(
        [
            lower_part * cosine - upper_part * sine_value,
            upper_part * cosine + lower_part * sine_value,
            vectors[..., ROT:],
        ],
        axis=-1,
    )


def restore_rows(block, row_count, col_count):
    width = block.shape[1]
    shard_rows = block.shape[0] // (row_count * col_count)
    return (
        block.reshape(col_count, row_count, shard_rows, width)
        .transpose(1, 0, 2, 3)
        .reshape(row_count * col_count * shard_rows, width)
    )


def on_device(
    prompt_tokens,
    decode_tokens,
    norm_gain,
    norm_bias,
    project_weight,
    dense_weight,
    expand_weight,
    reduce_weight,
    key_cache,
    value_cache,
    prompt_lengths,
    cache_ages,
    slot_request,
):
    half_float = jnp.bfloat16
    row_count = lax.axis_size("row")
    col_count = lax.axis_size("col")

    def by_row_group(weight):
        local_rows, width = weight.shape
        return weight.astype(half_float).reshape(local_rows, row_count, width // row_count)

    def regroup(weights):
        joined = jnp.concatenate([by_row_group(w) for w in weights], axis=2)
        swapped = lax.all_to_all(joined, "row", split_axis=1, concat_axis=0, tiled=True)
        flat = swapped.reshape(swapped.shape[0], swapped.shape[2])
        gathered = lax.all_gather(flat, "col", axis=0, tiled=True)
        restored = restore_rows(gathered, row_count, col_count)
        pieces = []
        offset = 0
        for w in weights:
            width = w.shape[1] // row_count
            pieces.append(restored[:, offset:offset + width])
            offset += width
        return pieces

    w_project, w_dense = regroup((project_weight, dense_weight))
    w_expand, w_reduce = regroup((expand_weight, reduce_weight))
    local_joined = jnp.concatenate([prompt_tokens, decode_tokens], axis=0)
    spread = jnp.broadcast_to(local_joined[None], (row_count,) + local_joined.shape)
    swapped_rows = lax.all_to_all(spread, "row", split_axis=0, concat_axis=0, tiled=True)
    joined = swapped_rows.transpose(1, 0, 2).reshape(local_joined.shape[0], -1)
    prompt_full = joined[: prompt_tokens.shape[0]]
    decode_full = joined[prompt_tokens.shape[0]:]
    rows_prompt = prompt_full.shape[0]
    slot_local = decode_full.shape[0]
    prompt_count = rows_prompt // PLEN
    heads_local = w_dense.shape[1] // HD
    total_slots = slot_request.shape[0]
    scale = HD ** (-0.5)
    normed = layer_norm(joined, norm_gain, norm_bias)
    merged = jnp.dot(normed, w_project, preferred_element_type=jnp.float32)
    hidden = jax.nn.gelu(
        jnp.dot(normed, w_expand, preferred_element_type=jnp.float32), approximate=True
    ).astype(half_float)
    mlp_part = lax.dot_general(
        hidden, w_reduce, (((1,), (1,)), ((), ())), preferred_element_type=jnp.float32
    )
    places = jnp.arange(PLEN, dtype=jnp.int32)

    def prompt_block(items):
        block, length = items
        queries = rotary(block[:, :, 0], places).astype(half_float)
        keys_rot = rotary(block[:, :, 1], places).astype(half_float)
        values = block[:, :, 2].astype(half_float)
        scores = (
            jnp.einsum("qhd,khd->hqk", queries, keys_rot, preferred_element_type=jnp.float32)
            * scale
        )
        allowed = (places[None, :] <= places[:, None]) & (places[None, :] < length)
        scores = jnp.where(allowed[None], scores, NEG)
        top = jnp.max(scores, axis=-1, keepdims=True)
        raised = jnp.exp(scores - top)
        probs = (raised / jnp.sum(raised, axis=-1, keepdims=True)).astype(half_float)
        mixed = jnp.einsum("hqk,khd->qhd", probs, values, preferred_element_type=jnp.float32)
        return mixed.astype(half_float).reshape(PLEN, heads_local * HD)

    prompt_blocks = merged[:rows_prompt].reshape(prompt_count, PLEN, heads_local, 3, HD)
    prompt_mixed = lax.map(prompt_block, (prompt_blocks, prompt_lengths)).reshape(
        rows_prompt, heads_local * HD
    )
    col_index = lax.axis_index("col")
    first_slot = col_index * slot_local
    local_ids = first_slot + jnp.arange(slot_local, dtype=jnp.int32)
    own_request = lax.dynamic_slice_in_dim(slot_request, first_slot, slot_local)
    all_ids = jnp.arange(total_slots, dtype=jnp.int32)
    slot_match = own_request[:, None] == all_ids[None, :]
    slot_age = jnp.sum(jnp.where(slot_match, cache_ages[None, :], 0), axis=1)
    decode_pieces = merged[rows_prompt:].reshape(slot_local, heads_local, 3, HD)
    query_new = rotary(decode_pieces[:, :, 0], slot_age).astype(half_float)
    key_new = rotary(decode_pieces[:, :, 1], slot_age).astype(half_float)
    value_new = decode_pieces[:, :, 2].astype(half_float)
    packed = jnp.stack([query_new, key_new, value_new], axis=2).reshape(
        slot_local, heads_local * 3 * HD
    )
    handed = lax.all_to_all(
        jnp.broadcast_to(packed, (col_count,) + packed.shape[1:]),
        "col", split_axis=0, concat_axis=0, tiled=True,
    )
    chooser = (slot_request[None, :] == local_ids[:, None]).astype(half_float)
    mine = jnp.dot(chooser, handed, preferred_element_type=jnp.float32).astype(half_float)
    mine = mine.reshape(slot_local, heads_local, 3, HD)
    query = mine[:, :, 0]
    own_key = mine[:, :, 1]
    own_value = mine[:, :, 2]
    local_ages = lax.dynamic_slice_in_dim(cache_ages, first_slot, slot_local)
    keys_local = key_cache.reshape(slot_local, heads_local, CTX, HD)
    values_local = value_cache.reshape(slot_local, heads_local, CTX, HD)
    block_count = CTX // KEY_BLOCK

    def score_block(step, held):
        start = step * KEY_BLOCK
        keys_block = lax.dynamic_slice_in_dim(keys_local, start, KEY_BLOCK, 2)
        block_scores = (
            jnp.einsum("shd,shtd->sht", query, keys_block, preferred_element_type=jnp.float32)
            * scale
        )
        key_places = start + jnp.arange(KEY_BLOCK, dtype=jnp.int32)
        block_scores = jnp.where(
            key_places[None, None, :] < local_ages[:, None, None], block_scores, NEG
        )
        return lax.dynamic_update_slice_in_dim(held, block_scores, start, 2)

    cache_scores = lax.fori_loop(
        0, block_count, score_block, jnp.full((slot_local, heads_local, CTX), NEG, jnp.float32)
    )
    own_score = jnp.sum(query.astype(jnp.float32) * own_key.astype(jnp.float32), axis=-1) * scale
    decode_top = jnp.maximum(jnp.max(cache_scores, axis=-1), own_score)
    cache_raised = jnp.exp(cache_scores - decode_top[:, :, None])
    own_raised = jnp.exp(own_score - decode_top)
    decode_total = jnp.sum(cache_raised, axis=-1) + own_raised
    cache_probs = (cache_raised / decode_total[:, :, None]).astype(half_float)
    own_prob = (own_raised / decode_total).astype(half_float)

    def value_block(step, running):
        start = step * KEY_BLOCK
        probs_block = lax.dynamic_slice_in_dim(cache_probs, start, KEY_BLOCK, 2)
        values_block = lax.dynamic_slice_in_dim(values_local, start, KEY_BLOCK, 2)
        return running + jnp.einsum(
            "sht,shtd->shd", probs_block, values_block, preferred_element_type=jnp.float32
        )

    start_value = own_prob.astype(jnp.float32)[:, :, None] * own_value.astype(jnp.float32)
    decode_sum = lax.fori_loop(0, block_count, value_block, start_value)
    decode_mixed = decode_sum.astype(half_float).reshape(slot_local, heads_local * HD)
    returned = lax.all_to_all(
        jnp.broadcast_to(decode_mixed, (col_count,) + decode_mixed.shape[1:]),
        "col", split_axis=0, concat_axis=0, tiled=True,
    )
    picker = slot_match.astype(half_float)
    decode_heads = jnp.dot(picker, returned, preferred_element_type=jnp.float32).astype(half_float)
    mixed_all = jnp.concatenate([prompt_mixed, decode_heads], axis=0)
    attn_part = lax.dot_general(
        mixed_all, w_dense, (((1,), (1,)), ((), ())), preferred_element_type=jnp.float32
    )
    summed = lax.psum_scatter(
        (attn_part + mlp_part).astype(half_float), "row", scatter_dimension=1, tiled=True
    ).astype(jnp.float32)
    prompt_result = prompt_tokens.astype(jnp.float32) + summed[:rows_prompt]
    decode_result = decode_tokens.astype(jnp.float32) + summed[rows_prompt:]
    return (prompt_result.astype(half_float), decode_result.astype(half_float))


def solution(mesh):
    in_specs = (
        P("col", "row"),
        P("col", "row"),
        P(),
        P(),
        P(("row", "col"), None),
        P(("row", "col"), None),
        P(("row", "col"), None),
        P(("row", "col"), None),
        P("col", "row", None),
        P("col", "row", None),
        P("col"),
        P(),
        P(),
    )
    out_specs = (P("col", "row"), P("col", "row"))
    return jax.shard_map(
        on_device, mesh=mesh, in_specs=in_specs, out_specs=out_specs, check_vma=False
    )
```

```python
import jax
import jax.numpy as jnp
from jax import lax
from jax.sharding import PartitionSpec as P

HD = 64
ROT = 32
PLEN = 512
CTX = 4096


NEG = -1e30


def layer_norm(rows, gain, bias):
    values = rows.astype(jnp.float32)
    centre = jnp.mean(values, axis=-1, keepdims=True)
    centred = values - centre
    deviation = jnp.mean(centred * centred, axis=-1, keepdims=True)
    return (centred * lax.rsqrt(deviation + 1e-05) * gain + bias).astype(jnp.bfloat16)


def rotary(vectors, position):
    half_width = ROT // 2
    frequency = 10000.0 ** (-2.0 * jnp.arange(half_width).astype(jnp.float32) / ROT)
    angle = position.astype(jnp.float32)[..., None, None] * frequency
    cosine = jnp.cos(angle)
    sine_value = jnp.sin(angle)
    lower_part = vectors[..., :half_width]
    upper_part = vectors[..., half_width:ROT]
    return jnp.concatenate(
        [
            lower_part * cosine - upper_part * sine_value,
            upper_part * cosine + lower_part * sine_value,
            vectors[..., ROT:],
        ],
        axis=-1,
    )


def on_device(
    prompt_tokens,
    decode_tokens,
    norm_gain,
    norm_bias,
    project_weight,
    dense_weight,
    expand_weight,
    reduce_weight,
    key_cache,
    value_cache,
    prompt_lengths,
    cache_ages,
    slot_request,
):
    half_float = jnp.bfloat16
    row_count = lax.axis_size("row")
    col_count = lax.axis_size("col")

    def by_row_group(weight):
        local_rows, width = weight.shape
        return weight.astype(half_float).reshape(local_rows, row_count, width // row_count)

    def regroup(weights):
        joined = jnp.concatenate([by_row_group(w) for w in weights], axis=2)
        swapped = lax.all_to_all(joined, "row", split_axis=1, concat_axis=0, tiled=True)
        flat = swapped.reshape(swapped.shape[0], swapped.shape[2])
        gathered = lax.all_gather(flat, "col", axis=0, tiled=True)
        pieces = []
        offset = 0
        for w in weights:
            width = w.shape[1] // row_count
            pieces.append(gathered[:, offset:offset + width])
            offset += width
        return pieces

    def to_gathered(values):
        lead = values.shape[:-1]
        return (
            values.reshape(lead + (row_count, col_count, -1))
            .swapaxes(-3, -2)
            .reshape(lead + (-1,))
        )

    def from_gathered(values):
        lead = values.shape[:-1]
        return (
            values.reshape(lead + (col_count, row_count, -1))
            .swapaxes(-3, -2)
            .reshape(lead + (-1,))
        )

    w_project, w_dense = regroup((project_weight, dense_weight))
    w_expand, w_reduce = regroup((expand_weight, reduce_weight))
    local_joined = jnp.concatenate([prompt_tokens, decode_tokens], axis=0)
    row_index = lax.axis_index("row")
    shifted = [local_joined] + [
        lax.ppermute(
            local_joined, "row", [(j, (j + k) % row_count) for j in range(row_count)]
        )
        for k in range(1, row_count)
    ]
    relative = jnp.stack(shifted, axis=0)
    blocks = jnp.stack(
        [
            lax.dynamic_index_in_dim(relative, (row_index - r) % row_count, 0, keepdims=False)
            for r in range(row_count)
        ],
        axis=0,
    )
    joined = (
        blocks.reshape(row_count, local_joined.shape[0], col_count, -1)
        .transpose(1, 2, 0, 3)
        .reshape(local_joined.shape[0], -1)
    )
    norm_gain = to_gathered(norm_gain)
    norm_bias = to_gathered(norm_bias)
    prompt_full = joined[: prompt_tokens.shape[0]]
    decode_full = joined[prompt_tokens.shape[0]:]
    rows_prompt = prompt_full.shape[0]
    slot_local = decode_full.shape[0]
    prompt_count = rows_prompt // PLEN
    heads_local = w_dense.shape[1] // HD
    total_slots = slot_request.shape[0]
    scale = HD ** (-0.5)
    normed = layer_norm(joined, norm_gain, norm_bias)
    merged = jnp.dot(normed, w_project, preferred_element_type=jnp.float32)
    hidden = jax.nn.gelu(
        jnp.dot(normed, w_expand, preferred_element_type=jnp.float32), approximate=True
    ).astype(half_float)
    mlp_part = lax.dot_general(
        hidden, w_reduce, (((1,), (1,)), ((), ())), preferred_element_type=jnp.float32
    )
    places = jnp.arange(PLEN, dtype=jnp.int32)

    def prompt_block(items):
        block, length = items
        queries = rotary(block[:, :, 0], places).astype(half_float)
        keys_rot = rotary(block[:, :, 1], places).astype(half_float)
        values = block[:, :, 2].astype(half_float)
        scores = (
            jnp.einsum("qhd,khd->hqk", queries, keys_rot, preferred_element_type=jnp.float32)
            * scale
        )
        allowed = (places[None, :] <= places[:, None]) & (places[None, :] < length)
        scores = jnp.where(allowed[None], scores, NEG)
        top = jnp.max(scores, axis=-1, keepdims=True)
        raised = jnp.exp(scores - top)
        probs = (raised / jnp.sum(raised, axis=-1, keepdims=True)).astype(half_float)
        mixed = jnp.einsum("hqk,khd->qhd", probs, values, preferred_element_type=jnp.float32)
        return mixed.astype(half_float).reshape(PLEN, heads_local * HD)

    prompt_blocks = merged[:rows_prompt].reshape(prompt_count, PLEN, heads_local, 3, HD)
    prompt_mixed = lax.map(prompt_block, (prompt_blocks, prompt_lengths)).reshape(
        rows_prompt, heads_local * HD
    )
    col_index = lax.axis_index("col")
    first_slot = col_index * slot_local
    local_ids = first_slot + jnp.arange(slot_local, dtype=jnp.int32)
    own_request = lax.dynamic_slice_in_dim(slot_request, first_slot, slot_local)
    all_ids = jnp.arange(total_slots, dtype=jnp.int32)
    slot_match = own_request[:, None] == all_ids[None, :]
    slot_age = jnp.sum(jnp.where(slot_match, cache_ages[None, :], 0), axis=1)
    decode_pieces = merged[rows_prompt:].reshape(slot_local, heads_local, 3, HD)
    query_new = rotary(decode_pieces[:, :, 0], slot_age).astype(half_float)
    key_new = rotary(decode_pieces[:, :, 1], slot_age).astype(half_float)
    value_new = decode_pieces[:, :, 2].astype(half_float)
    packed = jnp.stack([query_new, key_new, value_new], axis=2).reshape(
        slot_local, heads_local * 3 * HD
    )
    handed = lax.all_to_all(
        jnp.broadcast_to(packed, (col_count,) + packed.shape[1:]),
        "col", split_axis=0, concat_axis=0, tiled=True,
    )
    chooser = (slot_request[None, :] == local_ids[:, None]).astype(half_float)
    mine = jnp.dot(chooser, handed, preferred_element_type=jnp.float32).astype(half_float)
    mine = mine.reshape(slot_local, heads_local, 3, HD)
    query = mine[:, :, 0]
    own_key = mine[:, :, 1]
    own_value = mine[:, :, 2]
    local_ages = lax.dynamic_slice_in_dim(cache_ages, first_slot, slot_local)
    keys_local = key_cache.reshape(slot_local, heads_local, CTX, HD)
    values_local = value_cache.reshape(slot_local, heads_local, CTX, HD)
    cache_scores = (
        jnp.einsum("shd,shtd->sht", query, keys_local, preferred_element_type=jnp.float32) * scale
    )
    key_places = jnp.arange(CTX, dtype=jnp.int32)
    cache_scores = jnp.where(
        key_places[None, None, :] < local_ages[:, None, None], cache_scores, NEG
    )
    own_score = jnp.sum(query.astype(jnp.float32) * own_key.astype(jnp.float32), axis=-1) * scale
    decode_top = jnp.maximum(jnp.max(cache_scores, axis=-1), own_score)
    cache_raised = jnp.exp(cache_scores - decode_top[:, :, None])
    own_raised = jnp.exp(own_score - decode_top)
    decode_total = jnp.sum(cache_raised, axis=-1) + own_raised
    cache_probs = (cache_raised / decode_total[:, :, None]).astype(half_float)
    own_prob = (own_raised / decode_total).astype(half_float)

    start_value = own_prob.astype(jnp.float32)[:, :, None] * own_value.astype(jnp.float32)
    decode_sum = start_value + jnp.einsum(
        "sht,shtd->shd", cache_probs, values_local, preferred_element_type=jnp.float32
    )
    decode_mixed = decode_sum.astype(half_float).reshape(slot_local, heads_local * HD)
    returned = lax.all_to_all(
        jnp.broadcast_to(decode_mixed, (col_count,) + decode_mixed.shape[1:]),
        "col", split_axis=0, concat_axis=0, tiled=True,
    )
    picker = slot_match.astype(half_float)
    decode_heads = jnp.dot(picker, returned, preferred_element_type=jnp.float32).astype(half_float)
    mixed_all = jnp.concatenate([prompt_mixed, decode_heads], axis=0)
    attn_part = lax.dot_general(
        mixed_all, w_dense, (((1,), (1,)), ((), ())), preferred_element_type=jnp.float32
    )
    summed = lax.psum_scatter(
        from_gathered(attn_part + mlp_part).astype(half_float), "row", scatter_dimension=1, tiled=True
    ).astype(jnp.float32)
    prompt_result = prompt_tokens.astype(jnp.float32) + summed[:rows_prompt]
    decode_result = decode_tokens.astype(jnp.float32) + summed[rows_prompt:]
    return (prompt_result.astype(half_float), decode_result.astype(half_float))


def solution(mesh):
    in_specs = (
        P("col", "row"),
        P("col", "row"),
        P(),
        P(),
        P(("row", "col"), None),
        P(("row", "col"), None),
        P(("row", "col"), None),
        P(("row", "col"), None),
        P("col", "row", None),
        P("col", "row", None),
        P("col"),
        P(),
        P(),
    )
    out_specs = (P("col", "row"), P("col", "row"))
    return jax.shard_map(
        on_device, mesh=mesh, in_specs=in_specs, out_specs=out_specs, check_vma=False
    )
```

```python
import jax
import jax.numpy as jnp
from jax import lax
from jax.sharding import PartitionSpec as P

HD = 64
ROT = 32
PLEN = 512
CTX = 4096


NEG = -1e30
COL = ("col_y", "col_z", "col_x")


def layer_norm(rows, gain, bias):
    values = rows.astype(jnp.float32)
    centre = jnp.mean(values, axis=-1, keepdims=True)
    centred = values - centre
    deviation = jnp.mean(centred * centred, axis=-1, keepdims=True)
    return (centred * lax.rsqrt(deviation + 1e-05) * gain + bias).astype(jnp.bfloat16)


def rotary(vectors, position):
    half_width = ROT // 2
    frequency = 10000.0 ** (-2.0 * jnp.arange(half_width).astype(jnp.float32) / ROT)
    angle = position.astype(jnp.float32)[..., None, None] * frequency
    cosine = jnp.cos(angle)
    sine_value = jnp.sin(angle)
    lower_part = vectors[..., :half_width]
    upper_part = vectors[..., half_width:ROT]
    return jnp.concatenate(
        [
            lower_part * cosine - upper_part * sine_value,
            upper_part * cosine + lower_part * sine_value,
            vectors[..., ROT:],
        ],
        axis=-1,
    )


def on_device(
    prompt_tokens,
    decode_tokens,
    norm_gain,
    norm_bias,
    project_weight,
    dense_weight,
    expand_weight,
    reduce_weight,
    key_cache,
    value_cache,
    prompt_lengths,
    cache_ages,
    slot_request,
):
    half_float = jnp.bfloat16
    row_count = lax.axis_size("row")
    col_count = lax.axis_size(COL)

    def by_row_group(weight):
        local_rows, width = weight.shape
        return weight.astype(half_float).reshape(local_rows, row_count, width // row_count)

    def regroup(weights):
        joined = jnp.concatenate([by_row_group(w) for w in weights], axis=2)
        swapped = lax.all_to_all(joined, "row", split_axis=1, concat_axis=0, tiled=True)
        flat = swapped.reshape(swapped.shape[0], swapped.shape[2])
        gathered = lax.all_gather(flat, COL[-1], axis=0, tiled=True)
        gathered = lax.all_gather(gathered, COL[:-1], axis=0, tiled=True)
        pieces = []
        offset = 0
        for w in weights:
            width = w.shape[1] // row_count
            pieces.append(gathered[:, offset:offset + width])
            offset += width
        return pieces

    def to_gathered(values):
        lead = values.shape[:-1]
        return (
            values.reshape(lead + (row_count, col_count, -1))
            .swapaxes(-3, -2)
            .reshape(lead + (-1,))
        )

    def from_gathered(values):
        lead = values.shape[:-1]
        return (
            values.reshape(lead + (col_count, row_count, -1))
            .swapaxes(-3, -2)
            .reshape(lead + (-1,))
        )

    w_project, w_dense = regroup((project_weight, dense_weight))
    w_expand, w_reduce = regroup((expand_weight, reduce_weight))
    local_joined = jnp.concatenate([prompt_tokens, decode_tokens], axis=0)
    row_index = lax.axis_index("row")
    shifted = [local_joined] + [
        lax.ppermute(
            local_joined, "row", [(j, (j + k) % row_count) for j in range(row_count)]
        )
        for k in range(1, row_count)
    ]
    relative = jnp.stack(shifted, axis=0)
    blocks = jnp.stack(
        [
            lax.dynamic_index_in_dim(relative, (row_index - r) % row_count, 0, keepdims=False)
            for r in range(row_count)
        ],
        axis=0,
    )
    joined = (
        blocks.reshape(row_count, local_joined.shape[0], col_count, -1)
        .transpose(1, 2, 0, 3)
        .reshape(local_joined.shape[0], -1)
    )
    norm_gain = to_gathered(norm_gain)
    norm_bias = to_gathered(norm_bias)
    prompt_full = joined[: prompt_tokens.shape[0]]
    decode_full = joined[prompt_tokens.shape[0]:]
    rows_prompt = prompt_full.shape[0]
    slot_local = decode_full.shape[0]
    prompt_count = rows_prompt // PLEN
    heads_local = w_dense.shape[1] // HD
    total_slots = slot_request.shape[0]
    scale = HD ** (-0.5)
    normed = layer_norm(joined, norm_gain, norm_bias)
    merged = jnp.dot(normed, w_project, preferred_element_type=jnp.float32)
    hidden = jax.nn.gelu(
        jnp.dot(normed, w_expand, preferred_element_type=jnp.float32), approximate=True
    ).astype(half_float)
    mlp_part = lax.dot_general(
        hidden, w_reduce, (((1,), (1,)), ((), ())), preferred_element_type=jnp.float32
    )
    places = jnp.arange(PLEN, dtype=jnp.int32)

    def prompt_block(items):
        block, length = items
        queries = rotary(block[:, :, 0], places).astype(half_float)
        keys_rot = rotary(block[:, :, 1], places).astype(half_float)
        values = block[:, :, 2].astype(half_float)
        scores = (
            jnp.einsum("qhd,khd->hqk", queries, keys_rot, preferred_element_type=jnp.float32)
            * scale
        )
        allowed = (places[None, :] <= places[:, None]) & (places[None, :] < length)
        scores = jnp.where(allowed[None], scores, NEG)
        top = jnp.max(scores, axis=-1, keepdims=True)
        raised = jnp.exp(scores - top)
        probs = (raised / jnp.sum(raised, axis=-1, keepdims=True)).astype(half_float)
        mixed = jnp.einsum("hqk,khd->qhd", probs, values, preferred_element_type=jnp.float32)
        return mixed.astype(half_float).reshape(PLEN, heads_local * HD)

    prompt_blocks = merged[:rows_prompt].reshape(prompt_count, PLEN, heads_local, 3, HD)
    prompt_mixed = lax.map(prompt_block, (prompt_blocks, prompt_lengths)).reshape(
        rows_prompt, heads_local * HD
    )
    col_index = lax.axis_index(COL)
    first_slot = col_index * slot_local
    local_ids = first_slot + jnp.arange(slot_local, dtype=jnp.int32)
    own_request = lax.dynamic_slice_in_dim(slot_request, first_slot, slot_local)
    all_ids = jnp.arange(total_slots, dtype=jnp.int32)
    slot_match = own_request[:, None] == all_ids[None, :]
    slot_age = jnp.sum(jnp.where(slot_match, cache_ages[None, :], 0), axis=1)
    decode_pieces = merged[rows_prompt:].reshape(slot_local, heads_local, 3, HD)
    query_new = rotary(decode_pieces[:, :, 0], slot_age).astype(half_float)
    key_new = rotary(decode_pieces[:, :, 1], slot_age).astype(half_float)
    value_new = decode_pieces[:, :, 2].astype(half_float)
    packed = jnp.stack([query_new, key_new, value_new], axis=2).reshape(
        slot_local, heads_local * 3 * HD
    )
    handed = lax.all_to_all(
        jnp.broadcast_to(packed, (col_count,) + packed.shape[1:]),
        COL, split_axis=0, concat_axis=0, tiled=True,
    )
    chooser = (slot_request[None, :] == local_ids[:, None]).astype(half_float)
    mine = jnp.dot(chooser, handed, preferred_element_type=jnp.float32).astype(half_float)
    mine = mine.reshape(slot_local, heads_local, 3, HD)
    query = mine[:, :, 0]
    own_key = mine[:, :, 1]
    own_value = mine[:, :, 2]
    local_ages = lax.dynamic_slice_in_dim(cache_ages, first_slot, slot_local)
    keys_local = key_cache.reshape(slot_local, heads_local, CTX, HD)
    values_local = value_cache.reshape(slot_local, heads_local, CTX, HD)
    cache_scores = (
        jnp.einsum("shd,shtd->sht", query, keys_local, preferred_element_type=jnp.float32) * scale
    )
    key_places = jnp.arange(CTX, dtype=jnp.int32)
    cache_scores = jnp.where(
        key_places[None, None, :] < local_ages[:, None, None], cache_scores, NEG
    )
    own_score = jnp.sum(query.astype(jnp.float32) * own_key.astype(jnp.float32), axis=-1) * scale
    decode_top = jnp.maximum(jnp.max(cache_scores, axis=-1), own_score)
    cache_raised = jnp.exp(cache_scores - decode_top[:, :, None])
    own_raised = jnp.exp(own_score - decode_top)
    decode_total = jnp.sum(cache_raised, axis=-1) + own_raised
    cache_probs = (cache_raised / decode_total[:, :, None]).astype(half_float)
    own_prob = (own_raised / decode_total).astype(half_float)

    start_value = own_prob.astype(jnp.float32)[:, :, None] * own_value.astype(jnp.float32)
    decode_sum = start_value + jnp.einsum(
        "sht,shtd->shd", cache_probs, values_local, preferred_element_type=jnp.float32
    )
    decode_mixed = decode_sum.astype(half_float).reshape(slot_local, heads_local * HD)
    returned = lax.all_to_all(
        jnp.broadcast_to(decode_mixed, (col_count,) + decode_mixed.shape[1:]),
        COL, split_axis=0, concat_axis=0, tiled=True,
    )
    picker = slot_match.astype(half_float)
    decode_heads = jnp.dot(picker, returned, preferred_element_type=jnp.float32).astype(half_float)
    mixed_all = jnp.concatenate([prompt_mixed, decode_heads], axis=0)
    attn_part = lax.dot_general(
        mixed_all, w_dense, (((1,), (1,)), ((), ())), preferred_element_type=jnp.float32
    )
    summed = lax.psum_scatter(
        from_gathered(attn_part + mlp_part).astype(half_float), "row", scatter_dimension=1, tiled=True
    ).astype(jnp.float32)
    prompt_result = prompt_tokens.astype(jnp.float32) + summed[:rows_prompt]
    decode_result = decode_tokens.astype(jnp.float32) + summed[rows_prompt:]
    return (prompt_result.astype(half_float), decode_result.astype(half_float))


def solution(mesh):
    col_size = mesh.shape["col"]
    fine_mesh = jax.sharding.Mesh(
        mesh.devices.reshape(mesh.shape["row"], 4, col_size // 8, 2), ("row",) + COL
    )
    in_specs = (
        P(COL, "row"),
        P(COL, "row"),
        P(),
        P(),
        P(("row",) + COL, None),
        P(("row",) + COL, None),
        P(("row",) + COL, None),
        P(("row",) + COL, None),
        P(COL, "row", None),
        P(COL, "row", None),
        P(COL),
        P(),
        P(),
    )
    out_specs = (P(COL, "row"), P(COL, "row"))
    return jax.shard_map(
        on_device, mesh=fine_mesh, in_specs=in_specs, out_specs=out_specs, check_vma=False
    )
```

```python
import jax
import jax.numpy as jnp
from jax import lax
from jax.sharding import PartitionSpec as P

HD = 64
ROT = 32
PLEN = 512
CTX = 4096


NEG = -1e30
COL = ("col_y", "col_z", "col_x")


def layer_norm(rows, gain, bias):
    values = rows.astype(jnp.float32)
    centre = jnp.mean(values, axis=-1, keepdims=True)
    centred = values - centre
    deviation = jnp.mean(centred * centred, axis=-1, keepdims=True)
    return (centred * lax.rsqrt(deviation + 1e-05) * gain + bias).astype(jnp.bfloat16)


def rotary(vectors, position):
    half_width = ROT // 2
    frequency = 10000.0 ** (-2.0 * jnp.arange(half_width).astype(jnp.float32) / ROT)
    angle = position.astype(jnp.float32)[..., None, None] * frequency
    cosine = jnp.cos(angle)
    sine_value = jnp.sin(angle)
    lower_part = vectors[..., :half_width]
    upper_part = vectors[..., half_width:ROT]
    return jnp.concatenate(
        [
            lower_part * cosine - upper_part * sine_value,
            upper_part * cosine + lower_part * sine_value,
            vectors[..., ROT:],
        ],
        axis=-1,
    )


def on_device(
    prompt_tokens,
    decode_tokens,
    norm_gain,
    norm_bias,
    project_weight,
    dense_weight,
    expand_weight,
    reduce_weight,
    key_cache,
    value_cache,
    prompt_lengths,
    cache_ages,
    slot_request,
):
    half_float = jnp.bfloat16
    row_count = lax.axis_size("row")
    col_count = lax.axis_size(COL)

    def by_row_group(weight):
        local_rows, width = weight.shape
        return weight.astype(half_float).reshape(local_rows, row_count, width // row_count)

    def regroup(weights):
        joined = jnp.concatenate([by_row_group(w) for w in weights], axis=2)
        swapped = lax.all_to_all(joined, "row", split_axis=1, concat_axis=0, tiled=True)
        flat = swapped.reshape(swapped.shape[0], swapped.shape[2])
        gathered = lax.all_gather(flat, COL[-1], axis=0, tiled=True)
        gathered = lax.all_gather(gathered, COL[:-1], axis=0, tiled=True)
        pieces = []
        offset = 0
        for w in weights:
            width = w.shape[1] // row_count
            pieces.append(gathered[:, offset:offset + width])
            offset += width
        return pieces

    def to_gathered(values):
        lead = values.shape[:-1]
        return (
            values.reshape(lead + (row_count, col_count, -1))
            .swapaxes(-3, -2)
            .reshape(lead + (-1,))
        )

    def from_gathered(values):
        lead = values.shape[:-1]
        return (
            values.reshape(lead + (col_count, row_count, -1))
            .swapaxes(-3, -2)
            .reshape(lead + (-1,))
        )

    w_project, w_dense = regroup((project_weight, dense_weight))
    w_expand, w_reduce = regroup((expand_weight, reduce_weight))
    local_joined = jnp.concatenate([prompt_tokens, decode_tokens], axis=0)
    row_index = lax.axis_index("row")
    shifted = [local_joined] + [
        lax.ppermute(
            local_joined, "row", [(j, (j + k) % row_count) for j in range(row_count)]
        )
        for k in range(1, row_count)
    ]
    relative = jnp.stack(shifted, axis=0)
    blocks = jnp.stack(
        [
            lax.dynamic_index_in_dim(relative, (row_index - r) % row_count, 0, keepdims=False)
            for r in range(row_count)
        ],
        axis=0,
    )
    joined = (
        blocks.reshape(row_count, local_joined.shape[0], col_count, -1)
        .transpose(1, 2, 0, 3)
        .reshape(local_joined.shape[0], -1)
    )
    norm_gain = to_gathered(norm_gain)
    norm_bias = to_gathered(norm_bias)
    prompt_full = joined[: prompt_tokens.shape[0]]
    decode_full = joined[prompt_tokens.shape[0]:]
    rows_prompt = prompt_full.shape[0]
    slot_local = decode_full.shape[0]
    prompt_count = rows_prompt // PLEN
    heads_local = w_dense.shape[1] // HD
    total_slots = slot_request.shape[0]
    scale = HD ** (-0.5)
    normed = layer_norm(joined, norm_gain, norm_bias)
    merged = jnp.dot(normed, w_project, preferred_element_type=jnp.float32)
    places = jnp.arange(PLEN, dtype=jnp.int32)

    def prompt_block(items):
        block, length = items
        queries = rotary(block[:, :, 0], places).astype(half_float)
        keys_rot = rotary(block[:, :, 1], places).astype(half_float)
        values = block[:, :, 2].astype(half_float)
        scores = (
            jnp.einsum("qhd,khd->hqk", queries, keys_rot, preferred_element_type=jnp.float32)
            * scale
        )
        allowed = (places[None, :] <= places[:, None]) & (places[None, :] < length)
        scores = jnp.where(allowed[None], scores, NEG)
        top = jnp.max(scores, axis=-1, keepdims=True)
        raised = jnp.exp(scores - top)
        probs = (raised / jnp.sum(raised, axis=-1, keepdims=True)).astype(half_float)
        mixed = jnp.einsum("hqk,khd->qhd", probs, values, preferred_element_type=jnp.float32)
        return mixed.astype(half_float).reshape(PLEN, heads_local * HD)

    prompt_blocks = merged[:rows_prompt].reshape(prompt_count, PLEN, heads_local, 3, HD)
    prompt_mixed = lax.map(prompt_block, (prompt_blocks, prompt_lengths)).reshape(
        rows_prompt, heads_local * HD
    )
    col_index = lax.axis_index(COL)
    first_slot = col_index * slot_local
    local_ids = first_slot + jnp.arange(slot_local, dtype=jnp.int32)
    own_request = lax.dynamic_slice_in_dim(slot_request, first_slot, slot_local)
    all_ids = jnp.arange(total_slots, dtype=jnp.int32)
    slot_match = own_request[:, None] == all_ids[None, :]
    slot_age = jnp.sum(jnp.where(slot_match, cache_ages[None, :], 0), axis=1)
    decode_pieces = merged[rows_prompt:].reshape(slot_local, heads_local, 3, HD)
    query_new = rotary(decode_pieces[:, :, 0], slot_age).astype(half_float)
    key_new = rotary(decode_pieces[:, :, 1], slot_age).astype(half_float)
    value_new = decode_pieces[:, :, 2].astype(half_float)
    packed = jnp.stack([query_new, key_new, value_new], axis=2).reshape(
        slot_local, heads_local * 3 * HD
    )
    handed = lax.all_to_all(
        jnp.broadcast_to(packed, (col_count,) + packed.shape[1:]),
        COL, split_axis=0, concat_axis=0, tiled=True,
    )
    chooser = (slot_request[None, :] == local_ids[:, None]).astype(half_float)
    mine = jnp.dot(chooser, handed, preferred_element_type=jnp.float32).astype(half_float)
    mine = mine.reshape(slot_local, heads_local, 3, HD)
    query = mine[:, :, 0]
    own_key = mine[:, :, 1]
    own_value = mine[:, :, 2]
    local_ages = lax.dynamic_slice_in_dim(cache_ages, first_slot, slot_local)
    keys_local = key_cache.reshape(slot_local, heads_local, CTX, HD)
    values_local = value_cache.reshape(slot_local, heads_local, CTX, HD)
    cache_scores = (
        jnp.einsum("shd,shtd->sht", query, keys_local, preferred_element_type=jnp.float32) * scale
    )
    key_places = jnp.arange(CTX, dtype=jnp.int32)
    cache_scores = jnp.where(
        key_places[None, None, :] < local_ages[:, None, None], cache_scores, NEG
    )
    own_score = jnp.sum(query.astype(jnp.float32) * own_key.astype(jnp.float32), axis=-1) * scale
    decode_top = jnp.maximum(jnp.max(cache_scores, axis=-1), own_score)
    cache_raised = jnp.exp(cache_scores - decode_top[:, :, None])
    own_raised = jnp.exp(own_score - decode_top)
    decode_total = jnp.sum(cache_raised, axis=-1) + own_raised
    cache_probs = (cache_raised / decode_total[:, :, None]).astype(half_float)
    own_prob = (own_raised / decode_total).astype(half_float)

    start_value = own_prob.astype(jnp.float32)[:, :, None] * own_value.astype(jnp.float32)
    decode_sum = start_value + jnp.einsum(
        "sht,shtd->shd", cache_probs, values_local, preferred_element_type=jnp.float32
    )
    decode_mixed = decode_sum.astype(half_float).reshape(slot_local, heads_local * HD)
    returned = lax.all_to_all(
        jnp.broadcast_to(decode_mixed, (col_count,) + decode_mixed.shape[1:]),
        COL, split_axis=0, concat_axis=0, tiled=True,
    )
    picker = slot_match.astype(half_float)
    decode_heads = jnp.dot(picker, returned, preferred_element_type=jnp.float32).astype(half_float)
    mixed_all = jnp.concatenate([prompt_mixed, decode_heads], axis=0)
    attn_part = lax.dot_general(
        mixed_all, w_dense, (((1,), (1,)), ((), ())), preferred_element_type=jnp.float32
    )
    residual = jnp.concatenate([prompt_tokens, decode_tokens], axis=0)
    bounds = [0, rows_prompt // 2, normed.shape[0]]
    outputs = []
    for low, high in zip(bounds[:-1], bounds[1:]):
        hidden = jax.nn.gelu(
            jnp.dot(normed[low:high], w_expand, preferred_element_type=jnp.float32),
            approximate=True,
        ).astype(half_float)
        mlp_part = lax.dot_general(
            hidden, w_reduce, (((1,), (1,)), ((), ())), preferred_element_type=jnp.float32
        )
        summed = lax.psum_scatter(
            from_gathered(attn_part[low:high] + mlp_part).astype(half_float),
            "row",
            scatter_dimension=1,
            tiled=True,
        )
        outputs.append(
            (residual[low:high].astype(jnp.float32) + summed.astype(jnp.float32)).astype(half_float)
        )
    result = jnp.concatenate(outputs, axis=0)
    return (result[:rows_prompt], result[rows_prompt:])


def solution(mesh):
    col_size = mesh.shape["col"]
    fine_mesh = jax.sharding.Mesh(
        mesh.devices.reshape(mesh.shape["row"], 4, col_size // 8, 2), ("row",) + COL
    )
    in_specs = (
        P(COL, "row"),
        P(COL, "row"),
        P(),
        P(),
        P(("row",) + COL, None),
        P(("row",) + COL, None),
        P(("row",) + COL, None),
        P(("row",) + COL, None),
        P(COL, "row", None),
        P(COL, "row", None),
        P(COL),
        P(),
        P(),
    )
    out_specs = (P(COL, "row"), P(COL, "row"))
    return jax.shard_map(
        on_device, mesh=fine_mesh, in_specs=in_specs, out_specs=out_specs, check_vma=False
    )
```

```python
import functools

import jax
import jax.numpy as jnp
from jax import lax
from jax.experimental import pallas as pl
from jax.experimental.pallas import tpu as pltpu
from jax.sharding import PartitionSpec as P

HD = 64
ROT = 32
PLEN = 512
CTX = 4096


NEG = -1e30
COL = ("col_y", "col_z", "col_x")


def layer_norm(rows, gain, bias):
    values = rows.astype(jnp.float32)
    centre = jnp.mean(values, axis=-1, keepdims=True)
    centred = values - centre
    deviation = jnp.mean(centred * centred, axis=-1, keepdims=True)
    return (centred * lax.rsqrt(deviation + 1e-05) * gain + bias).astype(jnp.bfloat16)


def rotary(vectors, position):
    half_width = ROT // 2
    frequency = 10000.0 ** (-2.0 * jnp.arange(half_width).astype(jnp.float32) / ROT)
    angle = position.astype(jnp.float32)[..., None, None] * frequency
    cosine = jnp.cos(angle)
    sine_value = jnp.sin(angle)
    lower_part = vectors[..., :half_width]
    upper_part = vectors[..., half_width:ROT]
    return jnp.concatenate(
        [
            lower_part * cosine - upper_part * sine_value,
            upper_part * cosine + lower_part * sine_value,
            vectors[..., ROT:],
        ],
        axis=-1,
    )


def attention_kernel(lengths_ref, query_ref, key_ref, value_ref, out_ref, *, heads):
    length = lengths_ref[pl.program_id(0)]
    rows = lax.broadcasted_iota(jnp.int32, (PLEN, PLEN), 0)
    cols = lax.broadcasted_iota(jnp.int32, (PLEN, PLEN), 1)
    allowed = (cols <= rows) & (cols < length)
    for head in range(heads):
        lanes = slice(head * HD, (head + 1) * HD)
        scores = lax.dot_general(
            query_ref[:, lanes], key_ref[:, lanes], (((1,), (1,)), ((), ())),
            preferred_element_type=jnp.float32,
        ) * (HD ** -0.5)
        scores = jnp.where(allowed, scores, NEG)
        top = jnp.max(scores, axis=-1, keepdims=True)
        raised = jnp.exp(scores - top)
        probs = (raised / jnp.sum(raised, axis=-1, keepdims=True)).astype(jnp.bfloat16)
        mixed = jnp.dot(probs, value_ref[:, lanes], preferred_element_type=jnp.float32)
        out_ref[:, lanes] = mixed.astype(jnp.bfloat16)


def prompt_attention(lengths, queries, keys, values, heads, interpret=False):
    rows, width = queries.shape
    block = pl.BlockSpec((PLEN, width), lambda p, lengths_ref: (p, 0))
    return pl.pallas_call(
        functools.partial(attention_kernel, heads=heads),
        out_shape=jax.ShapeDtypeStruct((rows, width), jnp.bfloat16),
        grid_spec=pltpu.PrefetchScalarGridSpec(
            num_scalar_prefetch=1,
            grid=(rows // PLEN,),
            in_specs=[block, block, block],
            out_specs=block,
        ),
        interpret=interpret,
    )(lengths, queries, keys, values)


def on_device(
    prompt_tokens,
    decode_tokens,
    norm_gain,
    norm_bias,
    project_weight,
    dense_weight,
    expand_weight,
    reduce_weight,
    key_cache,
    value_cache,
    prompt_lengths,
    cache_ages,
    slot_request,
):
    half_float = jnp.bfloat16
    row_count = lax.axis_size("row")
    col_count = lax.axis_size(COL)

    def by_row_group(weight):
        local_rows, width = weight.shape
        return weight.astype(half_float).reshape(local_rows, row_count, width // row_count)

    def regroup(weights):
        joined = jnp.concatenate([by_row_group(w) for w in weights], axis=2)
        swapped = lax.all_to_all(joined, "row", split_axis=1, concat_axis=0, tiled=True)
        flat = swapped.reshape(swapped.shape[0], swapped.shape[2])
        gathered = lax.all_gather(flat, COL[-1], axis=0, tiled=True)
        gathered = lax.all_gather(gathered, COL[:-1], axis=0, tiled=True)
        pieces = []
        offset = 0
        for w in weights:
            width = w.shape[1] // row_count
            pieces.append(gathered[:, offset:offset + width])
            offset += width
        return pieces

    def to_gathered(values):
        lead = values.shape[:-1]
        return (
            values.reshape(lead + (row_count, col_count, -1))
            .swapaxes(-3, -2)
            .reshape(lead + (-1,))
        )

    def from_gathered(values):
        lead = values.shape[:-1]
        return (
            values.reshape(lead + (col_count, row_count, -1))
            .swapaxes(-3, -2)
            .reshape(lead + (-1,))
        )

    w_project, w_dense = regroup((project_weight, dense_weight))
    w_expand, w_reduce = regroup((expand_weight, reduce_weight))
    local_joined = jnp.concatenate([prompt_tokens, decode_tokens], axis=0)
    row_index = lax.axis_index("row")
    shifted = [local_joined] + [
        lax.ppermute(
            local_joined, "row", [(j, (j + k) % row_count) for j in range(row_count)]
        )
        for k in range(1, row_count)
    ]
    relative = jnp.stack(shifted, axis=0)
    blocks = jnp.stack(
        [
            lax.dynamic_index_in_dim(relative, (row_index - r) % row_count, 0, keepdims=False)
            for r in range(row_count)
        ],
        axis=0,
    )
    joined = (
        blocks.reshape(row_count, local_joined.shape[0], col_count, -1)
        .transpose(1, 2, 0, 3)
        .reshape(local_joined.shape[0], -1)
    )
    norm_gain = to_gathered(norm_gain)
    norm_bias = to_gathered(norm_bias)
    prompt_full = joined[: prompt_tokens.shape[0]]
    decode_full = joined[prompt_tokens.shape[0]:]
    rows_prompt = prompt_full.shape[0]
    slot_local = decode_full.shape[0]
    prompt_count = rows_prompt // PLEN
    heads_local = w_dense.shape[1] // HD
    total_slots = slot_request.shape[0]
    scale = HD ** (-0.5)
    normed = layer_norm(joined, norm_gain, norm_bias)
    merged = jnp.dot(normed, w_project, preferred_element_type=jnp.float32)
    prompt_pieces = merged[:rows_prompt].reshape(rows_prompt, heads_local, 3, HD)
    places = jnp.arange(rows_prompt, dtype=jnp.int32) % PLEN
    width = heads_local * HD
    prompt_queries = rotary(prompt_pieces[:, :, 0], places).astype(half_float).reshape(rows_prompt, width)
    prompt_keys = rotary(prompt_pieces[:, :, 1], places).astype(half_float).reshape(rows_prompt, width)
    prompt_values = prompt_pieces[:, :, 2].astype(half_float).reshape(rows_prompt, width)
    prompt_mixed = prompt_attention(
        prompt_lengths, prompt_queries, prompt_keys, prompt_values, heads_local
    )
    col_index = lax.axis_index(COL)
    first_slot = col_index * slot_local
    local_ids = first_slot + jnp.arange(slot_local, dtype=jnp.int32)
    own_request = lax.dynamic_slice_in_dim(slot_request, first_slot, slot_local)
    all_ids = jnp.arange(total_slots, dtype=jnp.int32)
    slot_match = own_request[:, None] == all_ids[None, :]
    slot_age = jnp.sum(jnp.where(slot_match, cache_ages[None, :], 0), axis=1)
    decode_pieces = merged[rows_prompt:].reshape(slot_local, heads_local, 3, HD)
    query_new = rotary(decode_pieces[:, :, 0], slot_age).astype(half_float)
    key_new = rotary(decode_pieces[:, :, 1], slot_age).astype(half_float)
    value_new = decode_pieces[:, :, 2].astype(half_float)
    packed = jnp.stack([query_new, key_new, value_new], axis=2).reshape(
        slot_local, heads_local * 3 * HD
    )
    handed = lax.all_to_all(
        jnp.broadcast_to(packed, (col_count,) + packed.shape[1:]),
        COL, split_axis=0, concat_axis=0, tiled=True,
    )
    chooser = (slot_request[None, :] == local_ids[:, None]).astype(half_float)
    mine = jnp.dot(chooser, handed, preferred_element_type=jnp.float32).astype(half_float)
    mine = mine.reshape(slot_local, heads_local, 3, HD)
    query = mine[:, :, 0]
    own_key = mine[:, :, 1]
    own_value = mine[:, :, 2]
    local_ages = lax.dynamic_slice_in_dim(cache_ages, first_slot, slot_local)
    keys_local = key_cache.reshape(slot_local, heads_local, CTX, HD)
    values_local = value_cache.reshape(slot_local, heads_local, CTX, HD)
    cache_scores = (
        jnp.einsum("shd,shtd->sht", query, keys_local, preferred_element_type=jnp.float32) * scale
    )
    key_places = jnp.arange(CTX, dtype=jnp.int32)
    cache_scores = jnp.where(
        key_places[None, None, :] < local_ages[:, None, None], cache_scores, NEG
    )
    own_score = jnp.sum(query.astype(jnp.float32) * own_key.astype(jnp.float32), axis=-1) * scale
    decode_top = jnp.maximum(jnp.max(cache_scores, axis=-1), own_score)
    cache_raised = jnp.exp(cache_scores - decode_top[:, :, None])
    own_raised = jnp.exp(own_score - decode_top)
    decode_total = jnp.sum(cache_raised, axis=-1) + own_raised
    cache_probs = (cache_raised / decode_total[:, :, None]).astype(half_float)
    own_prob = (own_raised / decode_total).astype(half_float)

    start_value = own_prob.astype(jnp.float32)[:, :, None] * own_value.astype(jnp.float32)
    decode_sum = start_value + jnp.einsum(
        "sht,shtd->shd", cache_probs, values_local, preferred_element_type=jnp.float32
    )
    decode_mixed = decode_sum.astype(half_float).reshape(slot_local, heads_local * HD)
    returned = lax.all_to_all(
        jnp.broadcast_to(decode_mixed, (col_count,) + decode_mixed.shape[1:]),
        COL, split_axis=0, concat_axis=0, tiled=True,
    )
    picker = slot_match.astype(half_float)
    decode_heads = jnp.dot(picker, returned, preferred_element_type=jnp.float32).astype(half_float)
    mixed_all = jnp.concatenate([prompt_mixed, decode_heads], axis=0)
    attn_part = lax.dot_general(
        mixed_all, w_dense, (((1,), (1,)), ((), ())), preferred_element_type=jnp.float32
    )
    residual = jnp.concatenate([prompt_tokens, decode_tokens], axis=0)
    bounds = [0, rows_prompt // 2, normed.shape[0]]
    outputs = []
    for low, high in zip(bounds[:-1], bounds[1:]):
        hidden = jax.nn.gelu(
            jnp.dot(normed[low:high], w_expand, preferred_element_type=jnp.float32),
            approximate=True,
        ).astype(half_float)
        mlp_part = lax.dot_general(
            hidden, w_reduce, (((1,), (1,)), ((), ())), preferred_element_type=jnp.float32
        )
        summed = lax.psum_scatter(
            from_gathered(attn_part[low:high] + mlp_part).astype(half_float),
            "row",
            scatter_dimension=1,
            tiled=True,
        )
        outputs.append(
            (residual[low:high].astype(jnp.float32) + summed.astype(jnp.float32)).astype(half_float)
        )
    result = jnp.concatenate(outputs, axis=0)
    return (result[:rows_prompt], result[rows_prompt:])


def solution(mesh):
    col_size = mesh.shape["col"]
    fine_mesh = jax.sharding.Mesh(
        mesh.devices.reshape(mesh.shape["row"], 4, col_size // 8, 2), ("row",) + COL
    )
    in_specs = (
        P(COL, "row"),
        P(COL, "row"),
        P(),
        P(),
        P(("row",) + COL, None),
        P(("row",) + COL, None),
        P(("row",) + COL, None),
        P(("row",) + COL, None),
        P(COL, "row", None),
        P(COL, "row", None),
        P(COL),
        P(),
        P(),
    )
    out_specs = (P(COL, "row"), P(COL, "row"))
    return jax.shard_map(
        on_device, mesh=fine_mesh, in_specs=in_specs, out_specs=out_specs, check_vma=False
    )
```

```python
import functools

import jax
import jax.numpy as jnp
from jax import lax
from jax.experimental import pallas as pl
from jax.experimental.pallas import tpu as pltpu
from jax.sharding import PartitionSpec as P

HD = 64
ROT = 32
PLEN = 512
CTX = 4096


NEG = -1e30
COL = ("col_y", "col_z", "col_x")


def layer_norm(rows, gain, bias):
    values = rows.astype(jnp.float32)
    centre = jnp.mean(values, axis=-1, keepdims=True)
    centred = values - centre
    deviation = jnp.mean(centred * centred, axis=-1, keepdims=True)
    return (centred * lax.rsqrt(deviation + 1e-05) * gain + bias).astype(jnp.bfloat16)


def rotary(vectors, position):
    half_width = ROT // 2
    frequency = 10000.0 ** (-2.0 * jnp.arange(half_width).astype(jnp.float32) / ROT)
    angle = position.astype(jnp.float32)[..., None, None] * frequency
    cosine = jnp.cos(angle)
    sine_value = jnp.sin(angle)
    lower_part = vectors[..., :half_width]
    upper_part = vectors[..., half_width:ROT]
    return jnp.concatenate(
        [
            lower_part * cosine - upper_part * sine_value,
            upper_part * cosine + lower_part * sine_value,
            vectors[..., ROT:],
        ],
        axis=-1,
    )


def attention_kernel(lengths_ref, query_ref, key_ref, value_ref, out_ref, *, heads):
    length = lengths_ref[pl.program_id(0)]
    rows = lax.broadcasted_iota(jnp.int32, (PLEN, PLEN), 0)
    cols = lax.broadcasted_iota(jnp.int32, (PLEN, PLEN), 1)
    allowed = (cols <= rows) & (cols < length)
    for head in range(heads):
        lanes = slice(head * HD, (head + 1) * HD)
        scores = lax.dot_general(
            query_ref[:, lanes], key_ref[:, lanes], (((1,), (1,)), ((), ())),
            preferred_element_type=jnp.float32,
        ) * (HD ** -0.5)
        scores = jnp.where(allowed, scores, NEG)
        top = jnp.max(scores, axis=-1, keepdims=True)
        raised = jnp.exp(scores - top)
        probs = (raised / jnp.sum(raised, axis=-1, keepdims=True)).astype(jnp.bfloat16)
        mixed = jnp.dot(probs, value_ref[:, lanes], preferred_element_type=jnp.float32)
        out_ref[:, lanes] = mixed.astype(jnp.bfloat16)


def prompt_attention(lengths, queries, keys, values, heads, interpret=False):
    rows, width = queries.shape
    block = pl.BlockSpec((PLEN, width), lambda p, lengths_ref: (p, 0))
    return pl.pallas_call(
        functools.partial(attention_kernel, heads=heads),
        out_shape=jax.ShapeDtypeStruct((rows, width), jnp.bfloat16),
        grid_spec=pltpu.PrefetchScalarGridSpec(
            num_scalar_prefetch=1,
            grid=(rows // PLEN,),
            in_specs=[block, block, block],
            out_specs=block,
        ),
        interpret=interpret,
    )(lengths, queries, keys, values)


def on_device(
    prompt_tokens,
    decode_tokens,
    norm_gain,
    norm_bias,
    project_weight,
    dense_weight,
    expand_weight,
    reduce_weight,
    key_cache,
    value_cache,
    prompt_lengths,
    cache_ages,
    slot_request,
):
    half_float = jnp.bfloat16
    row_count = lax.axis_size("row")
    col_count = lax.axis_size(COL)

    def by_row_group(weight):
        local_rows, width = weight.shape
        return weight.astype(half_float).reshape(local_rows, row_count, width // row_count)

    def regroup(weights):
        joined = jnp.concatenate([by_row_group(w) for w in weights], axis=2)
        swapped = lax.all_to_all(joined, "row", split_axis=1, concat_axis=0, tiled=True)
        flat = swapped.reshape(swapped.shape[0], swapped.shape[2])
        partner = lax.ppermute(flat, COL[-1], [(0, 1), (1, 0)])
        first = lax.axis_index(COL[-1]) == 0
        paired = jnp.concatenate(
            [jnp.where(first, flat, partner), jnp.where(first, partner, flat)], axis=0
        )
        gathered = lax.all_gather(paired, COL[:-1], axis=0, tiled=True)
        pieces = []
        offset = 0
        for w in weights:
            width = w.shape[1] // row_count
            pieces.append(gathered[:, offset:offset + width])
            offset += width
        return pieces

    def to_gathered(values):
        lead = values.shape[:-1]
        return (
            values.reshape(lead + (row_count, col_count, -1))
            .swapaxes(-3, -2)
            .reshape(lead + (-1,))
        )

    def from_gathered(values):
        lead = values.shape[:-1]
        return (
            values.reshape(lead + (col_count, row_count, -1))
            .swapaxes(-3, -2)
            .reshape(lead + (-1,))
        )

    w_project, w_dense = regroup((project_weight, dense_weight))
    w_expand, w_reduce = regroup((expand_weight, reduce_weight))
    local_joined = jnp.concatenate([prompt_tokens, decode_tokens], axis=0)
    row_index = lax.axis_index("row")
    shifted = [local_joined] + [
        lax.ppermute(
            local_joined, "row", [(j, (j + k) % row_count) for j in range(row_count)]
        )
        for k in range(1, row_count)
    ]
    relative = jnp.stack(shifted, axis=0)
    blocks = jnp.stack(
        [
            lax.dynamic_index_in_dim(relative, (row_index - r) % row_count, 0, keepdims=False)
            for r in range(row_count)
        ],
        axis=0,
    )
    joined = (
        blocks.reshape(row_count, local_joined.shape[0], col_count, -1)
        .transpose(1, 2, 0, 3)
        .reshape(local_joined.shape[0], -1)
    )
    norm_gain = to_gathered(norm_gain)
    norm_bias = to_gathered(norm_bias)
    prompt_full = joined[: prompt_tokens.shape[0]]
    decode_full = joined[prompt_tokens.shape[0]:]
    rows_prompt = prompt_full.shape[0]
    slot_local = decode_full.shape[0]
    prompt_count = rows_prompt // PLEN
    heads_local = w_dense.shape[1] // HD
    total_slots = slot_request.shape[0]
    scale = HD ** (-0.5)
    normed = layer_norm(joined, norm_gain, norm_bias)
    merged = jnp.dot(normed, w_project, preferred_element_type=jnp.float32)
    prompt_pieces = merged[:rows_prompt].reshape(rows_prompt, heads_local, 3, HD)
    places = jnp.arange(rows_prompt, dtype=jnp.int32) % PLEN
    width = heads_local * HD
    prompt_queries = rotary(prompt_pieces[:, :, 0], places).astype(half_float).reshape(rows_prompt, width)
    prompt_keys = rotary(prompt_pieces[:, :, 1], places).astype(half_float).reshape(rows_prompt, width)
    prompt_values = prompt_pieces[:, :, 2].astype(half_float).reshape(rows_prompt, width)
    prompt_mixed = prompt_attention(
        prompt_lengths, prompt_queries, prompt_keys, prompt_values, heads_local
    )
    col_index = lax.axis_index(COL)
    first_slot = col_index * slot_local
    local_ids = first_slot + jnp.arange(slot_local, dtype=jnp.int32)
    own_request = lax.dynamic_slice_in_dim(slot_request, first_slot, slot_local)
    all_ids = jnp.arange(total_slots, dtype=jnp.int32)
    slot_match = own_request[:, None] == all_ids[None, :]
    slot_age = jnp.sum(jnp.where(slot_match, cache_ages[None, :], 0), axis=1)
    decode_pieces = merged[rows_prompt:].reshape(slot_local, heads_local, 3, HD)
    query_new = rotary(decode_pieces[:, :, 0], slot_age).astype(half_float)
    key_new = rotary(decode_pieces[:, :, 1], slot_age).astype(half_float)
    value_new = decode_pieces[:, :, 2].astype(half_float)
    packed = jnp.stack([query_new, key_new, value_new], axis=2).reshape(
        slot_local, heads_local * 3 * HD
    )
    handed = lax.all_to_all(
        jnp.broadcast_to(packed, (col_count,) + packed.shape[1:]),
        COL, split_axis=0, concat_axis=0, tiled=True,
    )
    chooser = (slot_request[None, :] == local_ids[:, None]).astype(half_float)
    mine = jnp.dot(chooser, handed, preferred_element_type=jnp.float32).astype(half_float)
    mine = mine.reshape(slot_local, heads_local, 3, HD)
    query = mine[:, :, 0]
    own_key = mine[:, :, 1]
    own_value = mine[:, :, 2]
    local_ages = lax.dynamic_slice_in_dim(cache_ages, first_slot, slot_local)
    keys_local = key_cache.reshape(slot_local, heads_local, CTX, HD)
    values_local = value_cache.reshape(slot_local, heads_local, CTX, HD)
    cache_scores = (
        jnp.einsum("shd,shtd->sht", query, keys_local, preferred_element_type=jnp.float32) * scale
    )
    key_places = jnp.arange(CTX, dtype=jnp.int32)
    cache_scores = jnp.where(
        key_places[None, None, :] < local_ages[:, None, None], cache_scores, NEG
    )
    own_score = jnp.sum(query.astype(jnp.float32) * own_key.astype(jnp.float32), axis=-1) * scale
    decode_top = jnp.maximum(jnp.max(cache_scores, axis=-1), own_score)
    cache_raised = jnp.exp(cache_scores - decode_top[:, :, None])
    own_raised = jnp.exp(own_score - decode_top)
    decode_total = jnp.sum(cache_raised, axis=-1) + own_raised
    cache_probs = (cache_raised / decode_total[:, :, None]).astype(half_float)
    own_prob = (own_raised / decode_total).astype(half_float)

    start_value = own_prob.astype(jnp.float32)[:, :, None] * own_value.astype(jnp.float32)
    decode_sum = start_value + jnp.einsum(
        "sht,shtd->shd", cache_probs, values_local, preferred_element_type=jnp.float32
    )
    decode_mixed = decode_sum.astype(half_float).reshape(slot_local, heads_local * HD)
    returned = lax.all_to_all(
        jnp.broadcast_to(decode_mixed, (col_count,) + decode_mixed.shape[1:]),
        COL, split_axis=0, concat_axis=0, tiled=True,
    )
    picker = slot_match.astype(half_float)
    decode_heads = jnp.dot(picker, returned, preferred_element_type=jnp.float32).astype(half_float)
    mixed_all = jnp.concatenate([prompt_mixed, decode_heads], axis=0)
    attn_part = lax.dot_general(
        mixed_all, w_dense, (((1,), (1,)), ((), ())), preferred_element_type=jnp.float32
    )
    residual = jnp.concatenate([prompt_tokens, decode_tokens], axis=0)
    bounds = [0, rows_prompt // 4, rows_prompt // 2, 3 * rows_prompt // 4, normed.shape[0]]
    outputs = []
    for low, high in zip(bounds[:-1], bounds[1:]):
        hidden = jax.nn.gelu(
            jnp.dot(normed[low:high], w_expand, preferred_element_type=jnp.float32),
            approximate=True,
        ).astype(half_float)
        mlp_part = lax.dot_general(
            hidden, w_reduce, (((1,), (1,)), ((), ())), preferred_element_type=jnp.float32
        )
        summed = lax.psum_scatter(
            from_gathered(attn_part[low:high] + mlp_part).astype(half_float),
            "row",
            scatter_dimension=1,
            tiled=True,
        )
        outputs.append(
            (residual[low:high].astype(jnp.float32) + summed.astype(jnp.float32)).astype(half_float)
        )
    result = jnp.concatenate(outputs, axis=0)
    return (result[:rows_prompt], result[rows_prompt:])


def solution(mesh):
    col_size = mesh.shape["col"]
    fine_mesh = jax.sharding.Mesh(
        mesh.devices.reshape(mesh.shape["row"], 4, col_size // 8, 2), ("row",) + COL
    )
    in_specs = (
        P(COL, "row"),
        P(COL, "row"),
        P(),
        P(),
        P(("row",) + COL, None),
        P(("row",) + COL, None),
        P(("row",) + COL, None),
        P(("row",) + COL, None),
        P(COL, "row", None),
        P(COL, "row", None),
        P(COL),
        P(),
        P(),
    )
    out_specs = (P(COL, "row"), P(COL, "row"))
    return jax.shard_map(
        on_device, mesh=fine_mesh, in_specs=in_specs, out_specs=out_specs, check_vma=False
    )
```

```python
import functools

import jax
import jax.numpy as jnp
from jax import lax
from jax.experimental import pallas as pl
from jax.experimental.pallas import tpu as pltpu
from jax.sharding import PartitionSpec as P

HD = 64
ROT = 32
PLEN = 512
CTX = 4096


NEG = -1e30
COL = ("col_y", "col_z", "col_x")
ROW = ("row_x", "row_core")


def layer_norm(rows, gain, bias):
    values = rows.astype(jnp.float32)
    centre = jnp.mean(values, axis=-1, keepdims=True)
    centred = values - centre
    deviation = jnp.mean(centred * centred, axis=-1, keepdims=True)
    return (centred * lax.rsqrt(deviation + 1e-05) * gain + bias).astype(jnp.bfloat16)


def rotary(vectors, position):
    half_width = ROT // 2
    frequency = 10000.0 ** (-2.0 * jnp.arange(half_width).astype(jnp.float32) / ROT)
    angle = position.astype(jnp.float32)[..., None, None] * frequency
    cosine = jnp.cos(angle)
    sine_value = jnp.sin(angle)
    lower_part = vectors[..., :half_width]
    upper_part = vectors[..., half_width:ROT]
    return jnp.concatenate(
        [
            lower_part * cosine - upper_part * sine_value,
            upper_part * cosine + lower_part * sine_value,
            vectors[..., ROT:],
        ],
        axis=-1,
    )


def attention_kernel(lengths_ref, query_ref, key_ref, value_ref, out_ref, *, heads):
    length = lengths_ref[pl.program_id(0)]
    rows = lax.broadcasted_iota(jnp.int32, (PLEN, PLEN), 0)
    cols = lax.broadcasted_iota(jnp.int32, (PLEN, PLEN), 1)
    allowed = (cols <= rows) & (cols < length)
    for head in range(heads):
        lanes = slice(head * HD, (head + 1) * HD)
        scores = lax.dot_general(
            query_ref[:, lanes], key_ref[:, lanes], (((1,), (1,)), ((), ())),
            preferred_element_type=jnp.float32,
        ) * (HD ** -0.5)
        scores = jnp.where(allowed, scores, NEG)
        top = jnp.max(scores, axis=-1, keepdims=True)
        raised = jnp.exp(scores - top)
        probs = (raised / jnp.sum(raised, axis=-1, keepdims=True)).astype(jnp.bfloat16)
        mixed = jnp.dot(probs, value_ref[:, lanes], preferred_element_type=jnp.float32)
        out_ref[:, lanes] = mixed.astype(jnp.bfloat16)


def prompt_attention(lengths, queries, keys, values, heads, interpret=False):
    rows, width = queries.shape
    block = pl.BlockSpec((PLEN, width), lambda p, lengths_ref: (p, 0))
    return pl.pallas_call(
        functools.partial(attention_kernel, heads=heads),
        out_shape=jax.ShapeDtypeStruct((rows, width), jnp.bfloat16),
        grid_spec=pltpu.PrefetchScalarGridSpec(
            num_scalar_prefetch=1,
            grid=(rows // PLEN,),
            in_specs=[block, block, block],
            out_specs=block,
        ),
        interpret=interpret,
    )(lengths, queries, keys, values)


def on_device(
    prompt_tokens,
    decode_tokens,
    norm_gain,
    norm_bias,
    project_weight,
    dense_weight,
    expand_weight,
    reduce_weight,
    key_cache,
    value_cache,
    prompt_lengths,
    cache_ages,
    slot_request,
):
    half_float = jnp.bfloat16
    row_count = lax.axis_size(ROW)
    col_count = lax.axis_size(COL)

    def by_row_group(weight):
        local_rows, width = weight.shape
        return weight.astype(half_float).reshape(local_rows, row_count, width // row_count)

    def regroup(weights):
        joined = jnp.concatenate([by_row_group(w) for w in weights], axis=2)
        swapped = lax.all_to_all(joined, ROW, split_axis=1, concat_axis=0, tiled=True)
        flat = swapped.reshape(swapped.shape[0], swapped.shape[2])
        partner = lax.ppermute(flat, COL[-1], [(0, 1), (1, 0)])
        first = lax.axis_index(COL[-1]) == 0
        paired = jnp.concatenate(
            [jnp.where(first, flat, partner), jnp.where(first, partner, flat)], axis=0
        )
        gathered = lax.all_gather(paired, COL[:-1], axis=0, tiled=True)
        pieces = []
        offset = 0
        for w in weights:
            width = w.shape[1] // row_count
            pieces.append(gathered[:, offset:offset + width])
            offset += width
        return pieces

    def to_gathered(values):
        lead = values.shape[:-1]
        return (
            values.reshape(lead + (row_count, col_count, -1))
            .swapaxes(-3, -2)
            .reshape(lead + (-1,))
        )

    def from_gathered(values):
        lead = values.shape[:-1]
        return (
            values.reshape(lead + (col_count, row_count, -1))
            .swapaxes(-3, -2)
            .reshape(lead + (-1,))
        )

    w_project, w_dense = regroup((project_weight, dense_weight))
    w_expand, w_reduce = regroup((expand_weight, reduce_weight))
    local_joined = jnp.concatenate([prompt_tokens, decode_tokens], axis=0)
    row_index = lax.axis_index(ROW)
    shifted = [local_joined] + [
        lax.ppermute(
            local_joined, ROW, [(j, (j + k) % row_count) for j in range(row_count)]
        )
        for k in range(1, row_count)
    ]
    relative = jnp.stack(shifted, axis=0)
    blocks = jnp.stack(
        [
            lax.dynamic_index_in_dim(relative, (row_index - r) % row_count, 0, keepdims=False)
            for r in range(row_count)
        ],
        axis=0,
    )
    joined = (
        blocks.reshape(row_count, local_joined.shape[0], col_count, -1)
        .transpose(1, 2, 0, 3)
        .reshape(local_joined.shape[0], -1)
    )
    norm_gain = to_gathered(norm_gain)
    norm_bias = to_gathered(norm_bias)
    prompt_full = joined[: prompt_tokens.shape[0]]
    decode_full = joined[prompt_tokens.shape[0]:]
    rows_prompt = prompt_full.shape[0]
    slot_local = decode_full.shape[0]
    prompt_count = rows_prompt // PLEN
    heads_local = w_dense.shape[1] // HD
    total_slots = slot_request.shape[0]
    scale = HD ** (-0.5)
    normed = layer_norm(joined, norm_gain, norm_bias)
    merged = jnp.dot(normed, w_project, preferred_element_type=jnp.float32)
    prompt_pieces = merged[:rows_prompt].reshape(rows_prompt, heads_local, 3, HD)
    places = jnp.arange(rows_prompt, dtype=jnp.int32) % PLEN
    width = heads_local * HD
    prompt_queries = rotary(prompt_pieces[:, :, 0], places).astype(half_float).reshape(rows_prompt, width)
    prompt_keys = rotary(prompt_pieces[:, :, 1], places).astype(half_float).reshape(rows_prompt, width)
    prompt_values = prompt_pieces[:, :, 2].astype(half_float).reshape(rows_prompt, width)
    prompt_mixed = prompt_attention(
        prompt_lengths, prompt_queries, prompt_keys, prompt_values, heads_local
    )
    col_index = lax.axis_index(COL)
    first_slot = col_index * slot_local
    local_ids = first_slot + jnp.arange(slot_local, dtype=jnp.int32)
    own_request = lax.dynamic_slice_in_dim(slot_request, first_slot, slot_local)
    all_ids = jnp.arange(total_slots, dtype=jnp.int32)
    slot_match = own_request[:, None] == all_ids[None, :]
    slot_age = jnp.sum(jnp.where(slot_match, cache_ages[None, :], 0), axis=1)
    decode_pieces = merged[rows_prompt:].reshape(slot_local, heads_local, 3, HD)
    query_new = rotary(decode_pieces[:, :, 0], slot_age).astype(half_float)
    key_new = rotary(decode_pieces[:, :, 1], slot_age).astype(half_float)
    value_new = decode_pieces[:, :, 2].astype(half_float)
    packed = jnp.stack([query_new, key_new, value_new], axis=2).reshape(
        slot_local, heads_local * 3 * HD
    )
    handed = lax.all_to_all(
        jnp.broadcast_to(packed, (col_count,) + packed.shape[1:]),
        COL, split_axis=0, concat_axis=0, tiled=True,
    )
    chooser = (slot_request[None, :] == local_ids[:, None]).astype(half_float)
    mine = jnp.dot(chooser, handed, preferred_element_type=jnp.float32).astype(half_float)
    mine = mine.reshape(slot_local, heads_local, 3, HD)
    query = mine[:, :, 0]
    own_key = mine[:, :, 1]
    own_value = mine[:, :, 2]
    local_ages = lax.dynamic_slice_in_dim(cache_ages, first_slot, slot_local)
    keys_local = key_cache.reshape(slot_local, heads_local, CTX, HD)
    values_local = value_cache.reshape(slot_local, heads_local, CTX, HD)
    cache_scores = (
        jnp.einsum("shd,shtd->sht", query, keys_local, preferred_element_type=jnp.float32) * scale
    )
    key_places = jnp.arange(CTX, dtype=jnp.int32)
    cache_scores = jnp.where(
        key_places[None, None, :] < local_ages[:, None, None], cache_scores, NEG
    )
    own_score = jnp.sum(query.astype(jnp.float32) * own_key.astype(jnp.float32), axis=-1) * scale
    decode_top = jnp.maximum(jnp.max(cache_scores, axis=-1), own_score)
    cache_raised = jnp.exp(cache_scores - decode_top[:, :, None])
    own_raised = jnp.exp(own_score - decode_top)
    decode_total = jnp.sum(cache_raised, axis=-1) + own_raised
    cache_probs = (cache_raised / decode_total[:, :, None]).astype(half_float)
    own_prob = (own_raised / decode_total).astype(half_float)

    start_value = own_prob.astype(jnp.float32)[:, :, None] * own_value.astype(jnp.float32)
    decode_sum = start_value + jnp.einsum(
        "sht,shtd->shd", cache_probs, values_local, preferred_element_type=jnp.float32
    )
    decode_mixed = decode_sum.astype(half_float).reshape(slot_local, heads_local * HD)
    returned = lax.all_to_all(
        jnp.broadcast_to(decode_mixed, (col_count,) + decode_mixed.shape[1:]),
        COL, split_axis=0, concat_axis=0, tiled=True,
    )
    picker = slot_match.astype(half_float)
    decode_heads = jnp.dot(picker, returned, preferred_element_type=jnp.float32).astype(half_float)
    mixed_all = jnp.concatenate([prompt_mixed, decode_heads], axis=0)
    attn_part = lax.dot_general(
        mixed_all, w_dense, (((1,), (1,)), ((), ())), preferred_element_type=jnp.float32
    )
    residual = jnp.concatenate([prompt_tokens, decode_tokens], axis=0)
    bounds = [0, rows_prompt // 2, normed.shape[0]]
    outputs = []
    for low, high in zip(bounds[:-1], bounds[1:]):
        hidden = jax.nn.gelu(
            jnp.dot(normed[low:high], w_expand, preferred_element_type=jnp.float32),
            approximate=True,
        ).astype(half_float)
        mlp_part = lax.dot_general(
            hidden, w_reduce, (((1,), (1,)), ((), ())), preferred_element_type=jnp.float32
        )
        chunk = (attn_part[low:high] + mlp_part).astype(half_float)
        chunk = chunk.reshape(high - low, col_count, 2, row_count // 2, -1)
        chunk = chunk.transpose(3, 2, 0, 1, 4).reshape(row_count // 2, 2, high - low, -1)
        chunk = lax.psum_scatter(chunk, ROW[1], scatter_dimension=0, tiled=True)
        chunk = lax.psum_scatter(chunk, ROW[0], scatter_dimension=1, tiled=True)
        summed = chunk.reshape(high - low, -1)
        outputs.append(
            (residual[low:high].astype(jnp.float32) + summed.astype(jnp.float32)).astype(half_float)
        )
    result = jnp.concatenate(outputs, axis=0)
    return (result[:rows_prompt], result[rows_prompt:])


def solution(mesh):
    col_size = mesh.shape["col"]
    fine_mesh = jax.sharding.Mesh(
        mesh.devices.reshape(mesh.shape["row"] // 2, 2, 4, col_size // 8, 2), ROW + COL
    )
    in_specs = (
        P(COL, ROW),
        P(COL, ROW),
        P(),
        P(),
        P(ROW + COL, None),
        P(ROW + COL, None),
        P(ROW + COL, None),
        P(ROW + COL, None),
        P(COL, ROW, None),
        P(COL, ROW, None),
        P(COL),
        P(),
        P(),
    )
    out_specs = (P(COL, ROW), P(COL, ROW))
    return jax.shard_map(
        on_device, mesh=fine_mesh, in_specs=in_specs, out_specs=out_specs, check_vma=False
    )
```

```python
import functools

import jax
import jax.numpy as jnp
from jax import lax
from jax.experimental import pallas as pl
from jax.experimental.pallas import tpu as pltpu
from jax.sharding import PartitionSpec as P

HD = 64
ROT = 32
PLEN = 512
CTX = 4096


NEG = -1e30
COL = ("col_y", "col_z", "col_x")


def layer_norm(rows, gain, bias):
    values = rows.astype(jnp.float32)
    centre = jnp.mean(values, axis=-1, keepdims=True)
    centred = values - centre
    deviation = jnp.mean(centred * centred, axis=-1, keepdims=True)
    return (centred * lax.rsqrt(deviation + 1e-05) * gain + bias).astype(jnp.bfloat16)


def rotary(vectors, position):
    half_width = ROT // 2
    frequency = 10000.0 ** (-2.0 * jnp.arange(half_width).astype(jnp.float32) / ROT)
    angle = position.astype(jnp.float32)[..., None, None] * frequency
    cosine = jnp.cos(angle)
    sine_value = jnp.sin(angle)
    lower_part = vectors[..., :half_width]
    upper_part = vectors[..., half_width:ROT]
    return jnp.concatenate(
        [
            lower_part * cosine - upper_part * sine_value,
            upper_part * cosine + lower_part * sine_value,
            vectors[..., ROT:],
        ],
        axis=-1,
    )


def attention_kernel(lengths_ref, query_ref, key_ref, value_ref, out_ref, *, heads):
    length = lengths_ref[pl.program_id(0)]
    rows = lax.broadcasted_iota(jnp.int32, (PLEN, PLEN), 0)
    cols = lax.broadcasted_iota(jnp.int32, (PLEN, PLEN), 1)
    allowed = (cols <= rows) & (cols < length)
    for head in range(heads):
        lanes = slice(head * HD, (head + 1) * HD)
        scores = lax.dot_general(
            query_ref[:, lanes], key_ref[:, lanes], (((1,), (1,)), ((), ())),
            preferred_element_type=jnp.float32,
        ) * (HD ** -0.5)
        scores = jnp.where(allowed, scores, NEG)
        top = jnp.max(scores, axis=-1, keepdims=True)
        raised = jnp.exp(scores - top)
        probs = (raised / jnp.sum(raised, axis=-1, keepdims=True)).astype(jnp.bfloat16)
        mixed = jnp.dot(probs, value_ref[:, lanes], preferred_element_type=jnp.float32)
        out_ref[:, lanes] = mixed.astype(jnp.bfloat16)


def prompt_attention(lengths, queries, keys, values, heads, interpret=False):
    rows, width = queries.shape
    block = pl.BlockSpec((PLEN, width), lambda p, lengths_ref: (p, 0))
    return pl.pallas_call(
        functools.partial(attention_kernel, heads=heads),
        out_shape=jax.ShapeDtypeStruct((rows, width), jnp.bfloat16),
        grid_spec=pltpu.PrefetchScalarGridSpec(
            num_scalar_prefetch=1,
            grid=(rows // PLEN,),
            in_specs=[block, block, block],
            out_specs=block,
        ),
        interpret=interpret,
    )(lengths, queries, keys, values)


def on_device(
    prompt_tokens,
    decode_tokens,
    norm_gain,
    norm_bias,
    project_weight,
    dense_weight,
    expand_weight,
    reduce_weight,
    key_cache,
    value_cache,
    prompt_lengths,
    cache_ages,
    slot_request,
):
    half_float = jnp.bfloat16
    row_count = lax.axis_size("row")
    col_count = lax.axis_size(COL)

    def by_row_group(weight):
        local_rows, width = weight.shape
        return weight.astype(half_float).reshape(local_rows, row_count, width // row_count)

    def regroup(weights):
        joined = jnp.concatenate([by_row_group(w) for w in weights], axis=2)
        me = lax.axis_index("row")
        received = [lax.dynamic_index_in_dim(joined, me, 1, keepdims=False)] + [
            lax.ppermute(
                lax.dynamic_index_in_dim(joined, (me + k) % row_count, 1, keepdims=False),
                "row",
                [(j, (j + k) % row_count) for j in range(row_count)],
            )
            for k in range(1, row_count)
        ]
        by_source = jnp.stack(received, axis=0)
        flat = jnp.concatenate(
            [
                lax.dynamic_index_in_dim(by_source, (me - r) % row_count, 0, keepdims=False)
                for r in range(row_count)
            ],
            axis=0,
        )
        partner = lax.ppermute(flat, COL[-1], [(0, 1), (1, 0)])
        first = lax.axis_index(COL[-1]) == 0
        paired = jnp.concatenate(
            [jnp.where(first, flat, partner), jnp.where(first, partner, flat)], axis=0
        )
        gathered = lax.all_gather(paired, COL[:-1], axis=0, tiled=True)
        pieces = []
        offset = 0
        for w in weights:
            width = w.shape[1] // row_count
            pieces.append(gathered[:, offset:offset + width])
            offset += width
        return pieces

    def to_gathered(values):
        lead = values.shape[:-1]
        return (
            values.reshape(lead + (row_count, col_count, -1))
            .swapaxes(-3, -2)
            .reshape(lead + (-1,))
        )

    def from_gathered(values):
        lead = values.shape[:-1]
        return (
            values.reshape(lead + (col_count, row_count, -1))
            .swapaxes(-3, -2)
            .reshape(lead + (-1,))
        )

    w_project, w_dense = regroup((project_weight, dense_weight))
    w_expand, w_reduce = regroup((expand_weight, reduce_weight))
    local_joined = jnp.concatenate([prompt_tokens, decode_tokens], axis=0)
    row_index = lax.axis_index("row")
    shifted = [local_joined] + [
        lax.ppermute(
            local_joined, "row", [(j, (j + k) % row_count) for j in range(row_count)]
        )
        for k in range(1, row_count)
    ]
    relative = jnp.stack(shifted, axis=0)
    blocks = jnp.stack(
        [
            lax.dynamic_index_in_dim(relative, (row_index - r) % row_count, 0, keepdims=False)
            for r in range(row_count)
        ],
        axis=0,
    )
    joined = (
        blocks.reshape(row_count, local_joined.shape[0], col_count, -1)
        .transpose(1, 2, 0, 3)
        .reshape(local_joined.shape[0], -1)
    )
    norm_gain = to_gathered(norm_gain)
    norm_bias = to_gathered(norm_bias)
    prompt_full = joined[: prompt_tokens.shape[0]]
    decode_full = joined[prompt_tokens.shape[0]:]
    rows_prompt = prompt_full.shape[0]
    slot_local = decode_full.shape[0]
    prompt_count = rows_prompt // PLEN
    heads_local = w_dense.shape[1] // HD
    total_slots = slot_request.shape[0]
    scale = HD ** (-0.5)
    normed = layer_norm(joined, norm_gain, norm_bias)
    merged = jnp.dot(normed, w_project, preferred_element_type=jnp.float32)
    prompt_pieces = merged[:rows_prompt].reshape(rows_prompt, heads_local, 3, HD)
    places = jnp.arange(rows_prompt, dtype=jnp.int32) % PLEN
    width = heads_local * HD
    prompt_queries = rotary(prompt_pieces[:, :, 0], places).astype(half_float).reshape(rows_prompt, width)
    prompt_keys = rotary(prompt_pieces[:, :, 1], places).astype(half_float).reshape(rows_prompt, width)
    prompt_values = prompt_pieces[:, :, 2].astype(half_float).reshape(rows_prompt, width)
    prompt_mixed = prompt_attention(
        prompt_lengths, prompt_queries, prompt_keys, prompt_values, heads_local
    )
    col_index = lax.axis_index(COL)
    first_slot = col_index * slot_local
    local_ids = first_slot + jnp.arange(slot_local, dtype=jnp.int32)
    own_request = lax.dynamic_slice_in_dim(slot_request, first_slot, slot_local)
    all_ids = jnp.arange(total_slots, dtype=jnp.int32)
    slot_match = own_request[:, None] == all_ids[None, :]
    slot_age = jnp.sum(jnp.where(slot_match, cache_ages[None, :], 0), axis=1)
    decode_pieces = merged[rows_prompt:].reshape(slot_local, heads_local, 3, HD)
    query_new = rotary(decode_pieces[:, :, 0], slot_age).astype(half_float)
    key_new = rotary(decode_pieces[:, :, 1], slot_age).astype(half_float)
    value_new = decode_pieces[:, :, 2].astype(half_float)
    packed = jnp.stack([query_new, key_new, value_new], axis=2).reshape(
        slot_local, heads_local * 3 * HD
    )
    handed = lax.all_to_all(
        jnp.broadcast_to(packed, (col_count,) + packed.shape[1:]),
        COL, split_axis=0, concat_axis=0, tiled=True,
    )
    chooser = (slot_request[None, :] == local_ids[:, None]).astype(half_float)
    mine = jnp.dot(chooser, handed, preferred_element_type=jnp.float32).astype(half_float)
    mine = mine.reshape(slot_local, heads_local, 3, HD)
    query = mine[:, :, 0]
    own_key = mine[:, :, 1]
    own_value = mine[:, :, 2]
    local_ages = lax.dynamic_slice_in_dim(cache_ages, first_slot, slot_local)
    keys_local = key_cache.reshape(slot_local, heads_local, CTX, HD)
    values_local = value_cache.reshape(slot_local, heads_local, CTX, HD)
    cache_scores = (
        jnp.einsum("shd,shtd->sht", query, keys_local, preferred_element_type=jnp.float32) * scale
    )
    key_places = jnp.arange(CTX, dtype=jnp.int32)
    cache_scores = jnp.where(
        key_places[None, None, :] < local_ages[:, None, None], cache_scores, NEG
    )
    own_score = jnp.sum(query.astype(jnp.float32) * own_key.astype(jnp.float32), axis=-1) * scale
    decode_top = jnp.maximum(jnp.max(cache_scores, axis=-1), own_score)
    cache_raised = jnp.exp(cache_scores - decode_top[:, :, None])
    own_raised = jnp.exp(own_score - decode_top)
    decode_total = jnp.sum(cache_raised, axis=-1) + own_raised
    cache_probs = (cache_raised / decode_total[:, :, None]).astype(half_float)
    own_prob = (own_raised / decode_total).astype(half_float)

    start_value = own_prob.astype(jnp.float32)[:, :, None] * own_value.astype(jnp.float32)
    decode_sum = start_value + jnp.einsum(
        "sht,shtd->shd", cache_probs, values_local, preferred_element_type=jnp.float32
    )
    decode_mixed = decode_sum.astype(half_float).reshape(slot_local, heads_local * HD)
    returned = lax.all_to_all(
        jnp.broadcast_to(decode_mixed, (col_count,) + decode_mixed.shape[1:]),
        COL, split_axis=0, concat_axis=0, tiled=True,
    )
    picker = slot_match.astype(half_float)
    decode_heads = jnp.dot(picker, returned, preferred_element_type=jnp.float32).astype(half_float)
    mixed_all = jnp.concatenate([prompt_mixed, decode_heads], axis=0)
    attn_part = lax.dot_general(
        mixed_all, w_dense, (((1,), (1,)), ((), ())), preferred_element_type=jnp.float32
    )
    residual = jnp.concatenate([prompt_tokens, decode_tokens], axis=0)
    bounds = [0, rows_prompt // 2, normed.shape[0]]
    outputs = []
    for low, high in zip(bounds[:-1], bounds[1:]):
        hidden = jax.nn.gelu(
            jnp.dot(normed[low:high], w_expand, preferred_element_type=jnp.float32),
            approximate=True,
        ).astype(half_float)
        mlp_part = lax.dot_general(
            hidden, w_reduce, (((1,), (1,)), ((), ())), preferred_element_type=jnp.float32
        )
        summed = lax.psum_scatter(
            from_gathered(attn_part[low:high] + mlp_part).astype(half_float),
            "row",
            scatter_dimension=1,
            tiled=True,
        )
        outputs.append(
            (residual[low:high].astype(jnp.float32) + summed.astype(jnp.float32)).astype(half_float)
        )
    result = jnp.concatenate(outputs, axis=0)
    return (result[:rows_prompt], result[rows_prompt:])


def solution(mesh):
    col_size = mesh.shape["col"]
    fine_mesh = jax.sharding.Mesh(
        mesh.devices.reshape(mesh.shape["row"], 4, col_size // 8, 2), ("row",) + COL
    )
    in_specs = (
        P(COL, "row"),
        P(COL, "row"),
        P(),
        P(),
        P(("row",) + COL, None),
        P(("row",) + COL, None),
        P(("row",) + COL, None),
        P(("row",) + COL, None),
        P(COL, "row", None),
        P(COL, "row", None),
        P(COL),
        P(),
        P(),
    )
    out_specs = (P(COL, "row"), P(COL, "row"))
    return jax.shard_map(
        on_device, mesh=fine_mesh, in_specs=in_specs, out_specs=out_specs, check_vma=False
    )
```

```python
import functools

import jax
import jax.numpy as jnp
from jax import lax
from jax.experimental import pallas as pl
from jax.experimental.pallas import tpu as pltpu
from jax.sharding import PartitionSpec as P

HD = 64
ROT = 32
PLEN = 512
CTX = 4096


NEG = -1e30
COL = ("col_y", "col_z", "col_x")
ROW = ("row_x", "row_core")


def layer_norm(rows, gain, bias):
    values = rows.astype(jnp.float32)
    centre = jnp.mean(values, axis=-1, keepdims=True)
    centred = values - centre
    deviation = jnp.mean(centred * centred, axis=-1, keepdims=True)
    return (centred * lax.rsqrt(deviation + 1e-05) * gain + bias).astype(jnp.bfloat16)


def rotary(vectors, position):
    half_width = ROT // 2
    frequency = 10000.0 ** (-2.0 * jnp.arange(half_width).astype(jnp.float32) / ROT)
    angle = position.astype(jnp.float32)[..., None, None] * frequency
    cosine = jnp.cos(angle)
    sine_value = jnp.sin(angle)
    lower_part = vectors[..., :half_width]
    upper_part = vectors[..., half_width:ROT]
    return jnp.concatenate(
        [
            lower_part * cosine - upper_part * sine_value,
            upper_part * cosine + lower_part * sine_value,
            vectors[..., ROT:],
        ],
        axis=-1,
    )


def attention_kernel(lengths_ref, query_ref, key_ref, value_ref, out_ref, *, heads):
    length = lengths_ref[pl.program_id(0)]
    rows = lax.broadcasted_iota(jnp.int32, (PLEN, PLEN), 0)
    cols = lax.broadcasted_iota(jnp.int32, (PLEN, PLEN), 1)
    allowed = (cols <= rows) & (cols < length)
    for head in range(heads):
        lanes = slice(head * HD, (head + 1) * HD)
        scores = lax.dot_general(
            query_ref[:, lanes], key_ref[:, lanes], (((1,), (1,)), ((), ())),
            preferred_element_type=jnp.float32,
        ) * (HD ** -0.5)
        scores = jnp.where(allowed, scores, NEG)
        top = jnp.max(scores, axis=-1, keepdims=True)
        raised = jnp.exp(scores - top)
        probs = (raised / jnp.sum(raised, axis=-1, keepdims=True)).astype(jnp.bfloat16)
        mixed = jnp.dot(probs, value_ref[:, lanes], preferred_element_type=jnp.float32)
        out_ref[:, lanes] = mixed.astype(jnp.bfloat16)


def prompt_attention(lengths, queries, keys, values, heads, interpret=False):
    rows, width = queries.shape
    block = pl.BlockSpec((PLEN, width), lambda p, lengths_ref: (p, 0))
    return pl.pallas_call(
        functools.partial(attention_kernel, heads=heads),
        out_shape=jax.ShapeDtypeStruct((rows, width), jnp.bfloat16),
        grid_spec=pltpu.PrefetchScalarGridSpec(
            num_scalar_prefetch=1,
            grid=(rows // PLEN,),
            in_specs=[block, block, block],
            out_specs=block,
        ),
        interpret=interpret,
    )(lengths, queries, keys, values)


def on_device(
    prompt_tokens,
    decode_tokens,
    norm_gain,
    norm_bias,
    project_weight,
    dense_weight,
    expand_weight,
    reduce_weight,
    key_cache,
    value_cache,
    prompt_lengths,
    cache_ages,
    slot_request,
):
    half_float = jnp.bfloat16
    row_count = lax.axis_size(ROW)
    col_count = lax.axis_size(COL)

    def by_row_group(weight):
        local_rows, width = weight.shape
        return weight.astype(half_float).reshape(local_rows, row_count, width // row_count)

    def regroup(weights):
        joined = jnp.concatenate([by_row_group(w) for w in weights], axis=2)
        me = lax.axis_index(ROW)
        received = [lax.dynamic_index_in_dim(joined, me, 1, keepdims=False)] + [
            lax.ppermute(
                lax.dynamic_index_in_dim(joined, (me + k) % row_count, 1, keepdims=False),
                ROW,
                [(j, (j + k) % row_count) for j in range(row_count)],
            )
            for k in range(1, row_count)
        ]
        by_source = jnp.stack(received, axis=0)
        flat = jnp.concatenate(
            [
                lax.dynamic_index_in_dim(by_source, (me - r) % row_count, 0, keepdims=False)
                for r in range(row_count)
            ],
            axis=0,
        )
        partner = lax.ppermute(flat, COL[-1], [(0, 1), (1, 0)])
        first = lax.axis_index(COL[-1]) == 0
        paired = jnp.concatenate(
            [jnp.where(first, flat, partner), jnp.where(first, partner, flat)], axis=0
        )
        gathered = lax.all_gather(paired, COL[:-1], axis=0, tiled=True)
        pieces = []
        offset = 0
        for w in weights:
            width = w.shape[1] // row_count
            pieces.append(gathered[:, offset:offset + width])
            offset += width
        return pieces

    def to_gathered(values):
        lead = values.shape[:-1]
        return (
            values.reshape(lead + (row_count, col_count, -1))
            .swapaxes(-3, -2)
            .reshape(lead + (-1,))
        )

    def from_gathered(values):
        lead = values.shape[:-1]
        return (
            values.reshape(lead + (col_count, row_count, -1))
            .swapaxes(-3, -2)
            .reshape(lead + (-1,))
        )

    w_project, w_dense = regroup((project_weight, dense_weight))
    w_expand, w_reduce = regroup((expand_weight, reduce_weight))
    local_joined = jnp.concatenate([prompt_tokens, decode_tokens], axis=0)
    row_index = lax.axis_index(ROW)
    shifted = [local_joined] + [
        lax.ppermute(
            local_joined, ROW, [(j, (j + k) % row_count) for j in range(row_count)]
        )
        for k in range(1, row_count)
    ]
    relative = jnp.stack(shifted, axis=0)
    blocks = jnp.stack(
        [
            lax.dynamic_index_in_dim(relative, (row_index - r) % row_count, 0, keepdims=False)
            for r in range(row_count)
        ],
        axis=0,
    )
    joined = (
        blocks.reshape(row_count, local_joined.shape[0], col_count, -1)
        .transpose(1, 2, 0, 3)
        .reshape(local_joined.shape[0], -1)
    )
    norm_gain = to_gathered(norm_gain)
    norm_bias = to_gathered(norm_bias)
    prompt_full = joined[: prompt_tokens.shape[0]]
    decode_full = joined[prompt_tokens.shape[0]:]
    rows_prompt = prompt_full.shape[0]
    slot_local = decode_full.shape[0]
    prompt_count = rows_prompt // PLEN
    heads_local = w_dense.shape[1] // HD
    total_slots = slot_request.shape[0]
    scale = HD ** (-0.5)
    normed = layer_norm(joined, norm_gain, norm_bias)
    merged = jnp.dot(normed, w_project, preferred_element_type=jnp.float32)
    prompt_pieces = merged[:rows_prompt].reshape(rows_prompt, heads_local, 3, HD)
    places = jnp.arange(rows_prompt, dtype=jnp.int32) % PLEN
    width = heads_local * HD
    prompt_queries = rotary(prompt_pieces[:, :, 0], places).astype(half_float).reshape(rows_prompt, width)
    prompt_keys = rotary(prompt_pieces[:, :, 1], places).astype(half_float).reshape(rows_prompt, width)
    prompt_values = prompt_pieces[:, :, 2].astype(half_float).reshape(rows_prompt, width)
    prompt_mixed = prompt_attention(
        prompt_lengths, prompt_queries, prompt_keys, prompt_values, heads_local
    )
    col_index = lax.axis_index(COL)
    first_slot = col_index * slot_local
    local_ids = first_slot + jnp.arange(slot_local, dtype=jnp.int32)
    own_request = lax.dynamic_slice_in_dim(slot_request, first_slot, slot_local)
    all_ids = jnp.arange(total_slots, dtype=jnp.int32)
    slot_match = own_request[:, None] == all_ids[None, :]
    slot_age = jnp.sum(jnp.where(slot_match, cache_ages[None, :], 0), axis=1)
    decode_pieces = merged[rows_prompt:].reshape(slot_local, heads_local, 3, HD)
    query_new = rotary(decode_pieces[:, :, 0], slot_age).astype(half_float)
    key_new = rotary(decode_pieces[:, :, 1], slot_age).astype(half_float)
    value_new = decode_pieces[:, :, 2].astype(half_float)
    packed = jnp.stack([query_new, key_new, value_new], axis=2).reshape(
        slot_local, heads_local * 3 * HD
    )
    handed = lax.all_to_all(
        jnp.broadcast_to(packed, (col_count,) + packed.shape[1:]),
        COL, split_axis=0, concat_axis=0, tiled=True,
    )
    chooser = (slot_request[None, :] == local_ids[:, None]).astype(half_float)
    mine = jnp.dot(chooser, handed, preferred_element_type=jnp.float32).astype(half_float)
    mine = mine.reshape(slot_local, heads_local, 3, HD)
    query = mine[:, :, 0]
    own_key = mine[:, :, 1]
    own_value = mine[:, :, 2]
    local_ages = lax.dynamic_slice_in_dim(cache_ages, first_slot, slot_local)
    keys_local = key_cache.reshape(slot_local, heads_local, CTX, HD)
    values_local = value_cache.reshape(slot_local, heads_local, CTX, HD)
    cache_scores = (
        jnp.einsum("shd,shtd->sht", query, keys_local, preferred_element_type=jnp.float32) * scale
    )
    key_places = jnp.arange(CTX, dtype=jnp.int32)
    cache_scores = jnp.where(
        key_places[None, None, :] < local_ages[:, None, None], cache_scores, NEG
    )
    own_score = jnp.sum(query.astype(jnp.float32) * own_key.astype(jnp.float32), axis=-1) * scale
    decode_top = jnp.maximum(jnp.max(cache_scores, axis=-1), own_score)
    cache_raised = jnp.exp(cache_scores - decode_top[:, :, None])
    own_raised = jnp.exp(own_score - decode_top)
    decode_total = jnp.sum(cache_raised, axis=-1) + own_raised
    cache_probs = (cache_raised / decode_total[:, :, None]).astype(half_float)
    own_prob = (own_raised / decode_total).astype(half_float)

    start_value = own_prob.astype(jnp.float32)[:, :, None] * own_value.astype(jnp.float32)
    decode_sum = start_value + jnp.einsum(
        "sht,shtd->shd", cache_probs, values_local, preferred_element_type=jnp.float32
    )
    decode_mixed = decode_sum.astype(half_float).reshape(slot_local, heads_local * HD)
    returned = lax.all_to_all(
        jnp.broadcast_to(decode_mixed, (col_count,) + decode_mixed.shape[1:]),
        COL, split_axis=0, concat_axis=0, tiled=True,
    )
    picker = slot_match.astype(half_float)
    decode_heads = jnp.dot(picker, returned, preferred_element_type=jnp.float32).astype(half_float)
    mixed_all = jnp.concatenate([prompt_mixed, decode_heads], axis=0)
    attn_part = lax.dot_general(
        mixed_all, w_dense, (((1,), (1,)), ((), ())), preferred_element_type=jnp.float32
    )
    residual = jnp.concatenate([prompt_tokens, decode_tokens], axis=0)
    bounds = [0, rows_prompt // 2, normed.shape[0]]
    outputs = []
    for low, high in zip(bounds[:-1], bounds[1:]):
        hidden = jax.nn.gelu(
            jnp.dot(normed[low:high], w_expand, preferred_element_type=jnp.float32),
            approximate=True,
        ).astype(half_float)
        mlp_part = lax.dot_general(
            hidden, w_reduce, (((1,), (1,)), ((), ())), preferred_element_type=jnp.float32
        )
        chunk = from_gathered(attn_part[low:high] + mlp_part).astype(half_float)
        chunk = chunk.reshape(high - low, 2, row_count // 2, -1).transpose(2, 1, 0, 3)
        core = lax.axis_index(ROW[1])
        mine = lax.dynamic_index_in_dim(chunk, core, 0, keepdims=False)
        other = lax.dynamic_index_in_dim(chunk, 1 - core, 0, keepdims=False)
        pair_sum = (
            mine.astype(jnp.float32)
            + lax.ppermute(other, ROW[1], [(0, 1), (1, 0)]).astype(jnp.float32)
        ).astype(half_float)
        summed = lax.psum_scatter(pair_sum, ROW[0], scatter_dimension=0, tiled=True)
        summed = summed.reshape(high - low, -1)
        outputs.append(
            (residual[low:high].astype(jnp.float32) + summed.astype(jnp.float32)).astype(half_float)
        )
    result = jnp.concatenate(outputs, axis=0)
    return (result[:rows_prompt], result[rows_prompt:])


def solution(mesh):
    col_size = mesh.shape["col"]
    fine_mesh = jax.sharding.Mesh(
        mesh.devices.reshape(mesh.shape["row"] // 2, 2, 4, col_size // 8, 2), ROW + COL
    )
    in_specs = (
        P(COL, ROW),
        P(COL, ROW),
        P(),
        P(),
        P(ROW + COL, None),
        P(ROW + COL, None),
        P(ROW + COL, None),
        P(ROW + COL, None),
        P(COL, ROW, None),
        P(COL, ROW, None),
        P(COL),
        P(),
        P(),
    )
    out_specs = (P(COL, ROW), P(COL, ROW))
    return jax.shard_map(
        on_device, mesh=fine_mesh, in_specs=in_specs, out_specs=out_specs, check_vma=False
    )
```

```python
import functools

import jax
import jax.numpy as jnp
from jax import lax
from jax.experimental import pallas as pl
from jax.experimental.pallas import tpu as pltpu
from jax.sharding import PartitionSpec as P

HD = 64
ROT = 32
PLEN = 512
CTX = 4096


NEG = -1e30
COL = ("col_y", "col_z", "col_x")
ROW = ("row_x", "row_core")


def layer_norm(rows, gain, bias):
    values = rows.astype(jnp.float32)
    centre = jnp.mean(values, axis=-1, keepdims=True)
    centred = values - centre
    deviation = jnp.mean(centred * centred, axis=-1, keepdims=True)
    return (centred * lax.rsqrt(deviation + 1e-05) * gain + bias).astype(jnp.bfloat16)


def rotary(vectors, position):
    half_width = ROT // 2
    frequency = 10000.0 ** (-2.0 * jnp.arange(half_width).astype(jnp.float32) / ROT)
    angle = position.astype(jnp.float32)[..., None, None] * frequency
    cosine = jnp.cos(angle)
    sine_value = jnp.sin(angle)
    lower_part = vectors[..., :half_width]
    upper_part = vectors[..., half_width:ROT]
    return jnp.concatenate(
        [
            lower_part * cosine - upper_part * sine_value,
            upper_part * cosine + lower_part * sine_value,
            vectors[..., ROT:],
        ],
        axis=-1,
    )


def attention_kernel(lengths_ref, query_ref, key_ref, value_ref, out_ref, *, heads):
    length = lengths_ref[pl.program_id(0)]
    rows = lax.broadcasted_iota(jnp.int32, (PLEN, PLEN), 0)
    cols = lax.broadcasted_iota(jnp.int32, (PLEN, PLEN), 1)
    allowed = (cols <= rows) & (cols < length)
    for head in range(heads):
        lanes = slice(head * HD, (head + 1) * HD)
        scores = lax.dot_general(
            query_ref[:, lanes], key_ref[:, lanes], (((1,), (1,)), ((), ())),
            preferred_element_type=jnp.float32,
        ) * (HD ** -0.5)
        scores = jnp.where(allowed, scores, NEG)
        top = jnp.max(scores, axis=-1, keepdims=True)
        raised = jnp.exp(scores - top)
        probs = (raised / jnp.sum(raised, axis=-1, keepdims=True)).astype(jnp.bfloat16)
        mixed = jnp.dot(probs, value_ref[:, lanes], preferred_element_type=jnp.float32)
        out_ref[:, lanes] = mixed.astype(jnp.bfloat16)


def prompt_attention(lengths, queries, keys, values, heads, interpret=False):
    rows, width = queries.shape
    block = pl.BlockSpec((PLEN, width), lambda p, lengths_ref: (p, 0))
    return pl.pallas_call(
        functools.partial(attention_kernel, heads=heads),
        out_shape=jax.ShapeDtypeStruct((rows, width), jnp.bfloat16),
        grid_spec=pltpu.PrefetchScalarGridSpec(
            num_scalar_prefetch=1,
            grid=(rows // PLEN,),
            in_specs=[block, block, block],
            out_specs=block,
        ),
        interpret=interpret,
    )(lengths, queries, keys, values)


def on_device(
    prompt_tokens,
    decode_tokens,
    norm_gain,
    norm_bias,
    project_weight,
    dense_weight,
    expand_weight,
    reduce_weight,
    key_cache,
    value_cache,
    prompt_lengths,
    cache_ages,
    slot_request,
):
    half_float = jnp.bfloat16
    row_count = lax.axis_size(ROW)
    col_count = lax.axis_size(COL)

    def by_row_group(weight):
        local_rows, width = weight.shape
        return weight.astype(half_float).reshape(local_rows, row_count, width // row_count)

    def regroup(weights):
        joined = jnp.concatenate([by_row_group(w) for w in weights], axis=2)
        me = lax.axis_index(ROW)
        received = [lax.dynamic_index_in_dim(joined, me, 1, keepdims=False)] + [
            lax.ppermute(
                lax.dynamic_index_in_dim(joined, (me + k) % row_count, 1, keepdims=False),
                ROW,
                [(j, (j + k) % row_count) for j in range(row_count)],
            )
            for k in range(1, row_count)
        ]
        by_source = jnp.stack(received, axis=0)
        flat = jnp.concatenate(
            [
                lax.dynamic_index_in_dim(by_source, (me - r) % row_count, 0, keepdims=False)
                for r in range(row_count)
            ],
            axis=0,
        )
        partner = lax.ppermute(flat, COL[-1], [(0, 1), (1, 0)])
        first = lax.axis_index(COL[-1]) == 0
        paired = jnp.concatenate(
            [jnp.where(first, flat, partner), jnp.where(first, partner, flat)], axis=0
        )
        gathered = lax.all_gather(paired, COL[:-1], axis=0, tiled=True)
        pieces = []
        offset = 0
        for w in weights:
            width = w.shape[1] // row_count
            pieces.append(gathered[:, offset:offset + width])
            offset += width
        return pieces

    def to_gathered(values):
        lead = values.shape[:-1]
        return (
            values.reshape(lead + (row_count, col_count, -1))
            .swapaxes(-3, -2)
            .reshape(lead + (-1,))
        )

    def from_gathered(values):
        lead = values.shape[:-1]
        return (
            values.reshape(lead + (col_count, row_count, -1))
            .swapaxes(-3, -2)
            .reshape(lead + (-1,))
        )

    w_project, w_dense = regroup((project_weight, dense_weight))
    w_expand, w_reduce = regroup((expand_weight, reduce_weight))
    local_joined = jnp.concatenate([prompt_tokens, decode_tokens], axis=0)
    row_index = lax.axis_index(ROW)
    shifted = [local_joined] + [
        lax.ppermute(
            local_joined, ROW, [(j, (j + k) % row_count) for j in range(row_count)]
        )
        for k in range(1, row_count)
    ]
    relative = jnp.stack(shifted, axis=0)
    blocks = jnp.stack(
        [
            lax.dynamic_index_in_dim(relative, (row_index - r) % row_count, 0, keepdims=False)
            for r in range(row_count)
        ],
        axis=0,
    )
    joined = (
        blocks.reshape(row_count, local_joined.shape[0], col_count, -1)
        .transpose(1, 2, 0, 3)
        .reshape(local_joined.shape[0], -1)
    )
    norm_gain = to_gathered(norm_gain)
    norm_bias = to_gathered(norm_bias)
    prompt_full = joined[: prompt_tokens.shape[0]]
    decode_full = joined[prompt_tokens.shape[0]:]
    rows_prompt = prompt_full.shape[0]
    slot_local = decode_full.shape[0]
    prompt_count = rows_prompt // PLEN
    heads_local = w_dense.shape[1] // HD
    total_slots = slot_request.shape[0]
    scale = HD ** (-0.5)
    normed = layer_norm(joined, norm_gain, norm_bias)
    merged = jnp.dot(normed, w_project, preferred_element_type=jnp.float32)
    prompt_pieces = merged[:rows_prompt].reshape(rows_prompt, heads_local, 3, HD)
    places = jnp.arange(rows_prompt, dtype=jnp.int32) % PLEN
    width = heads_local * HD
    prompt_queries = rotary(prompt_pieces[:, :, 0], places).astype(half_float).reshape(rows_prompt, width)
    prompt_keys = rotary(prompt_pieces[:, :, 1], places).astype(half_float).reshape(rows_prompt, width)
    prompt_values = prompt_pieces[:, :, 2].astype(half_float).reshape(rows_prompt, width)
    prompt_mixed = prompt_attention(
        prompt_lengths, prompt_queries, prompt_keys, prompt_values, heads_local
    )
    col_index = lax.axis_index(COL)
    first_slot = col_index * slot_local
    local_ids = first_slot + jnp.arange(slot_local, dtype=jnp.int32)
    own_request = lax.dynamic_slice_in_dim(slot_request, first_slot, slot_local)
    all_ids = jnp.arange(total_slots, dtype=jnp.int32)
    slot_match = own_request[:, None] == all_ids[None, :]
    slot_age = jnp.sum(jnp.where(slot_match, cache_ages[None, :], 0), axis=1)
    decode_pieces = merged[rows_prompt:].reshape(slot_local, heads_local, 3, HD)
    query_new = rotary(decode_pieces[:, :, 0], slot_age).astype(half_float)
    key_new = rotary(decode_pieces[:, :, 1], slot_age).astype(half_float)
    value_new = decode_pieces[:, :, 2].astype(half_float)
    packed = jnp.stack([query_new, key_new, value_new], axis=2).reshape(
        slot_local, heads_local * 3 * HD
    )
    handed = lax.all_to_all(
        jnp.broadcast_to(packed, (col_count,) + packed.shape[1:]),
        COL, split_axis=0, concat_axis=0, tiled=True,
    )
    chooser = (slot_request[None, :] == local_ids[:, None]).astype(half_float)
    mine = jnp.dot(chooser, handed, preferred_element_type=jnp.float32).astype(half_float)
    mine = mine.reshape(slot_local, heads_local, 3, HD)
    query = mine[:, :, 0]
    own_key = mine[:, :, 1]
    own_value = mine[:, :, 2]
    local_ages = lax.dynamic_slice_in_dim(cache_ages, first_slot, slot_local)
    keys_local = key_cache.reshape(slot_local, heads_local, CTX, HD)
    values_local = value_cache.reshape(slot_local, heads_local, CTX, HD)
    cache_scores = (
        jnp.einsum("shd,shtd->sht", query, keys_local, preferred_element_type=jnp.float32) * scale
    )
    key_places = jnp.arange(CTX, dtype=jnp.int32)
    cache_scores = jnp.where(
        key_places[None, None, :] < local_ages[:, None, None], cache_scores, NEG
    )
    own_score = jnp.sum(query.astype(jnp.float32) * own_key.astype(jnp.float32), axis=-1) * scale
    decode_top = jnp.maximum(jnp.max(cache_scores, axis=-1), own_score)
    cache_raised = jnp.exp(cache_scores - decode_top[:, :, None])
    own_raised = jnp.exp(own_score - decode_top)
    decode_total = jnp.sum(cache_raised, axis=-1) + own_raised
    cache_probs = (cache_raised / decode_total[:, :, None]).astype(half_float)
    own_prob = (own_raised / decode_total).astype(half_float)

    start_value = own_prob.astype(jnp.float32)[:, :, None] * own_value.astype(jnp.float32)
    decode_sum = start_value + jnp.einsum(
        "sht,shtd->shd", cache_probs, values_local, preferred_element_type=jnp.float32
    )
    decode_mixed = decode_sum.astype(half_float).reshape(slot_local, heads_local * HD)
    returned = lax.all_to_all(
        jnp.broadcast_to(decode_mixed, (col_count,) + decode_mixed.shape[1:]),
        COL, split_axis=0, concat_axis=0, tiled=True,
    )
    picker = slot_match.astype(half_float)
    decode_heads = jnp.dot(picker, returned, preferred_element_type=jnp.float32).astype(half_float)
    mixed_all = jnp.concatenate([prompt_mixed, decode_heads], axis=0)
    attn_part = lax.dot_general(
        mixed_all, w_dense, (((1,), (1,)), ((), ())), preferred_element_type=jnp.float32
    )
    residual = jnp.concatenate([prompt_tokens, decode_tokens], axis=0)
    bounds = [0, 3 * rows_prompt // 8, 3 * rows_prompt // 4, normed.shape[0]]
    outputs = []
    for low, high in zip(bounds[:-1], bounds[1:]):
        hidden = jax.nn.gelu(
            jnp.dot(normed[low:high], w_expand, preferred_element_type=jnp.float32),
            approximate=True,
        ).astype(half_float)
        mlp_part = lax.dot_general(
            hidden, w_reduce, (((1,), (1,)), ((), ())), preferred_element_type=jnp.float32
        )
        chunk = from_gathered(attn_part[low:high] + mlp_part).astype(half_float)
        chunk = chunk.reshape(high - low, 2, row_count // 2, -1).transpose(2, 1, 0, 3)
        core = lax.axis_index(ROW[1])
        mine = lax.dynamic_index_in_dim(chunk, core, 0, keepdims=False)
        other = lax.dynamic_index_in_dim(chunk, 1 - core, 0, keepdims=False)
        pair_sum = (
            mine.astype(jnp.float32)
            + lax.ppermute(other, ROW[1], [(0, 1), (1, 0)]).astype(jnp.float32)
        ).astype(half_float)
        summed = lax.psum_scatter(pair_sum, ROW[0], scatter_dimension=0, tiled=True)
        summed = summed.reshape(high - low, -1)
        outputs.append(
            (residual[low:high].astype(jnp.float32) + summed.astype(jnp.float32)).astype(half_float)
        )
    result = jnp.concatenate(outputs, axis=0)
    return (result[:rows_prompt], result[rows_prompt:])


def solution(mesh):
    col_size = mesh.shape["col"]
    fine_mesh = jax.sharding.Mesh(
        mesh.devices.reshape(mesh.shape["row"] // 2, 2, 4, col_size // 8, 2), ROW + COL
    )
    in_specs = (
        P(COL, ROW),
        P(COL, ROW),
        P(),
        P(),
        P(ROW + COL, None),
        P(ROW + COL, None),
        P(ROW + COL, None),
        P(ROW + COL, None),
        P(COL, ROW, None),
        P(COL, ROW, None),
        P(COL),
        P(),
        P(),
    )
    out_specs = (P(COL, ROW), P(COL, ROW))
    return jax.shard_map(
        on_device, mesh=fine_mesh, in_specs=in_specs, out_specs=out_specs, check_vma=False
    )
```

```python
import functools

import jax
import jax.numpy as jnp
from jax import lax
from jax.experimental import pallas as pl
from jax.experimental.pallas import tpu as pltpu
from jax.sharding import PartitionSpec as P

HD = 64
ROT = 32
PLEN = 512
CTX = 4096


NEG = -1e30
COL = ("col_y", "col_z", "col_x")
ROW = ("row_x", "row_core")


def layer_norm(rows, gain, bias):
    values = rows.astype(jnp.float32)
    centre = jnp.mean(values, axis=-1, keepdims=True)
    centred = values - centre
    deviation = jnp.mean(centred * centred, axis=-1, keepdims=True)
    return (centred * lax.rsqrt(deviation + 1e-05) * gain + bias).astype(jnp.bfloat16)


def rotary(vectors, position):
    half_width = ROT // 2
    frequency = 10000.0 ** (-2.0 * jnp.arange(half_width).astype(jnp.float32) / ROT)
    angle = position.astype(jnp.float32)[..., None, None] * frequency
    cosine = jnp.cos(angle)
    sine_value = jnp.sin(angle)
    lower_part = vectors[..., :half_width]
    upper_part = vectors[..., half_width:ROT]
    return jnp.concatenate(
        [
            lower_part * cosine - upper_part * sine_value,
            upper_part * cosine + lower_part * sine_value,
            vectors[..., ROT:],
        ],
        axis=-1,
    )


def attention_kernel(lengths_ref, query_ref, key_ref, value_ref, out_ref, *, heads):
    length = lengths_ref[pl.program_id(0)]
    rows = lax.broadcasted_iota(jnp.int32, (PLEN, PLEN), 0)
    cols = lax.broadcasted_iota(jnp.int32, (PLEN, PLEN), 1)
    allowed = (cols <= rows) & (cols < length)
    for head in range(heads):
        lanes = slice(head * HD, (head + 1) * HD)
        scores = lax.dot_general(
            query_ref[:, lanes], key_ref[:, lanes], (((1,), (1,)), ((), ())),
            preferred_element_type=jnp.float32,
        ) * (HD ** -0.5)
        scores = jnp.where(allowed, scores, NEG)
        top = jnp.max(scores, axis=-1, keepdims=True)
        raised = jnp.exp(scores - top)
        probs = (raised / jnp.sum(raised, axis=-1, keepdims=True)).astype(jnp.bfloat16)
        mixed = jnp.dot(probs, value_ref[:, lanes], preferred_element_type=jnp.float32)
        out_ref[:, lanes] = mixed.astype(jnp.bfloat16)


def prompt_attention(lengths, queries, keys, values, heads, interpret=False):
    rows, width = queries.shape
    block = pl.BlockSpec((PLEN, width), lambda p, lengths_ref: (p, 0))
    return pl.pallas_call(
        functools.partial(attention_kernel, heads=heads),
        out_shape=jax.ShapeDtypeStruct((rows, width), jnp.bfloat16),
        grid_spec=pltpu.PrefetchScalarGridSpec(
            num_scalar_prefetch=1,
            grid=(rows // PLEN,),
            in_specs=[block, block, block],
            out_specs=block,
        ),
        interpret=interpret,
    )(lengths, queries, keys, values)


def on_device(
    prompt_tokens,
    decode_tokens,
    norm_gain,
    norm_bias,
    project_weight,
    dense_weight,
    expand_weight,
    reduce_weight,
    key_cache,
    value_cache,
    prompt_lengths,
    cache_ages,
    slot_request,
):
    half_float = jnp.bfloat16
    row_count = lax.axis_size(ROW)
    col_count = lax.axis_size(COL)

    def by_row_group(weight):
        local_rows, width = weight.shape
        return weight.astype(half_float).reshape(local_rows, row_count, width // row_count)

    def regroup(weights):
        joined = jnp.concatenate([by_row_group(w) for w in weights], axis=2)
        me = lax.axis_index(ROW)
        received = [lax.dynamic_index_in_dim(joined, me, 1, keepdims=False)] + [
            lax.ppermute(
                lax.dynamic_index_in_dim(joined, (me + k) % row_count, 1, keepdims=False),
                ROW,
                [(j, (j + k) % row_count) for j in range(row_count)],
            )
            for k in range(1, row_count)
        ]
        by_source = jnp.stack(received, axis=0)
        flat = jnp.concatenate(
            [
                lax.dynamic_index_in_dim(by_source, (me - r) % row_count, 0, keepdims=False)
                for r in range(row_count)
            ],
            axis=0,
        )
        partner = lax.ppermute(flat, COL[-1], [(0, 1), (1, 0)])
        first = lax.axis_index(COL[-1]) == 0
        paired = jnp.concatenate(
            [jnp.where(first, flat, partner), jnp.where(first, partner, flat)], axis=0
        )
        gathered = lax.all_gather(paired, COL[:-1], axis=0, tiled=True)
        pieces = []
        offset = 0
        for w in weights:
            width = w.shape[1] // row_count
            pieces.append(gathered[:, offset:offset + width])
            offset += width
        return pieces

    def to_gathered(values):
        lead = values.shape[:-1]
        return (
            values.reshape(lead + (row_count, col_count, -1))
            .swapaxes(-3, -2)
            .reshape(lead + (-1,))
        )

    def from_gathered(values):
        lead = values.shape[:-1]
        return (
            values.reshape(lead + (col_count, row_count, -1))
            .swapaxes(-3, -2)
            .reshape(lead + (-1,))
        )

    w_project, w_dense = regroup((project_weight, dense_weight))
    w_expand, w_reduce = regroup((expand_weight, reduce_weight))
    local_joined = jnp.concatenate([prompt_tokens, decode_tokens], axis=0)
    row_index = lax.axis_index(ROW)
    shifted = [local_joined] + [
        lax.ppermute(
            local_joined, ROW, [(j, (j + k) % row_count) for j in range(row_count)]
        )
        for k in range(1, row_count)
    ]
    relative = jnp.stack(shifted, axis=0)
    blocks = jnp.stack(
        [
            lax.dynamic_index_in_dim(relative, (row_index - r) % row_count, 0, keepdims=False)
            for r in range(row_count)
        ],
        axis=0,
    )
    joined = (
        blocks.reshape(row_count, local_joined.shape[0], col_count, -1)
        .transpose(1, 2, 0, 3)
        .reshape(local_joined.shape[0], -1)
    )
    norm_gain = to_gathered(norm_gain)
    norm_bias = to_gathered(norm_bias)
    prompt_full = joined[: prompt_tokens.shape[0]]
    decode_full = joined[prompt_tokens.shape[0]:]
    rows_prompt = prompt_full.shape[0]
    slot_local = decode_full.shape[0]
    prompt_count = rows_prompt // PLEN
    heads_local = w_dense.shape[1] // HD
    total_slots = slot_request.shape[0]
    scale = HD ** (-0.5)
    normed = layer_norm(joined, norm_gain, norm_bias)
    merged = jnp.dot(normed, w_project, preferred_element_type=jnp.float32)
    prompt_pieces = merged[:rows_prompt].reshape(rows_prompt, heads_local, 3, HD)
    places = jnp.arange(rows_prompt, dtype=jnp.int32) % PLEN
    width = heads_local * HD
    prompt_queries = rotary(prompt_pieces[:, :, 0], places).astype(half_float).reshape(rows_prompt, width)
    prompt_keys = rotary(prompt_pieces[:, :, 1], places).astype(half_float).reshape(rows_prompt, width)
    prompt_values = prompt_pieces[:, :, 2].astype(half_float).reshape(rows_prompt, width)
    prompt_mixed = prompt_attention(
        prompt_lengths, prompt_queries, prompt_keys, prompt_values, heads_local
    )
    col_index = lax.axis_index(COL)
    first_slot = col_index * slot_local
    local_ids = first_slot + jnp.arange(slot_local, dtype=jnp.int32)
    own_request = lax.dynamic_slice_in_dim(slot_request, first_slot, slot_local)
    all_ids = jnp.arange(total_slots, dtype=jnp.int32)
    slot_match = own_request[:, None] == all_ids[None, :]
    slot_age = jnp.sum(jnp.where(slot_match, cache_ages[None, :], 0), axis=1)
    decode_pieces = merged[rows_prompt:].reshape(slot_local, heads_local, 3, HD)
    query_new = rotary(decode_pieces[:, :, 0], slot_age).astype(half_float)
    key_new = rotary(decode_pieces[:, :, 1], slot_age).astype(half_float)
    value_new = decode_pieces[:, :, 2].astype(half_float)
    packed = jnp.stack([query_new, key_new, value_new], axis=2).reshape(
        slot_local, heads_local * 3 * HD
    )
    handed = lax.all_to_all(
        jnp.broadcast_to(packed, (col_count,) + packed.shape[1:]),
        COL, split_axis=0, concat_axis=0, tiled=True,
    )
    chooser = (slot_request[None, :] == local_ids[:, None]).astype(half_float)
    mine = jnp.dot(chooser, handed, preferred_element_type=jnp.float32).astype(half_float)
    mine = mine.reshape(slot_local, heads_local, 3, HD)
    query = mine[:, :, 0]
    own_key = mine[:, :, 1]
    own_value = mine[:, :, 2]
    local_ages = lax.dynamic_slice_in_dim(cache_ages, first_slot, slot_local)
    keys_local = key_cache.reshape(slot_local, heads_local, CTX, HD)
    values_local = value_cache.reshape(slot_local, heads_local, CTX, HD)
    cache_scores = (
        jnp.einsum("shd,shtd->sht", query, keys_local, preferred_element_type=jnp.float32) * scale
    )
    key_places = jnp.arange(CTX, dtype=jnp.int32)
    cache_scores = jnp.where(
        key_places[None, None, :] < local_ages[:, None, None], cache_scores, NEG
    )
    own_score = jnp.sum(query.astype(jnp.float32) * own_key.astype(jnp.float32), axis=-1) * scale
    decode_top = jnp.maximum(jnp.max(cache_scores, axis=-1), own_score)
    cache_raised = jnp.exp(cache_scores - decode_top[:, :, None])
    own_raised = jnp.exp(own_score - decode_top)
    decode_total = jnp.sum(cache_raised, axis=-1) + own_raised
    cache_probs = (cache_raised / decode_total[:, :, None]).astype(half_float)
    own_prob = (own_raised / decode_total).astype(half_float)

    start_value = own_prob.astype(jnp.float32)[:, :, None] * own_value.astype(jnp.float32)
    decode_sum = start_value + jnp.einsum(
        "sht,shtd->shd", cache_probs, values_local, preferred_element_type=jnp.float32
    )
    decode_mixed = decode_sum.astype(half_float).reshape(slot_local, heads_local * HD)
    returned = lax.all_to_all(
        jnp.broadcast_to(decode_mixed, (col_count,) + decode_mixed.shape[1:]),
        COL, split_axis=0, concat_axis=0, tiled=True,
    )
    picker = slot_match.astype(half_float)
    decode_heads = jnp.dot(picker, returned, preferred_element_type=jnp.float32).astype(half_float)
    mixed_all = jnp.concatenate([prompt_mixed, decode_heads], axis=0)
    attn_part = lax.dot_general(
        mixed_all, w_dense, (((1,), (1,)), ((), ())), preferred_element_type=jnp.float32
    )
    residual = jnp.concatenate([prompt_tokens, decode_tokens], axis=0)
    bounds = [0, rows_prompt // 2, normed.shape[0]]
    outputs = []
    for low, high in zip(bounds[:-1], bounds[1:]):
        hidden = jax.nn.gelu(
            jnp.dot(normed[low:high], w_expand, preferred_element_type=jnp.float32),
            approximate=True,
        ).astype(half_float)
        mlp_part = lax.dot_general(
            hidden, w_reduce, (((1,), (1,)), ((), ())), preferred_element_type=jnp.float32
        )
        chunk = from_gathered(attn_part[low:high] + mlp_part).astype(half_float)
        chunk = chunk.reshape(high - low, 2, row_count // 2, -1).transpose(2, 1, 0, 3)
        core = lax.axis_index(ROW[1])
        mine = lax.dynamic_index_in_dim(chunk, core, 0, keepdims=False)
        other = lax.dynamic_index_in_dim(chunk, 1 - core, 0, keepdims=False)
        pair_sum = (
            mine.astype(jnp.float32)
            + lax.ppermute(other, ROW[1], [(0, 1), (1, 0)]).astype(jnp.float32)
        ).astype(half_float)
        side = lax.axis_index(ROW[0])
        kept = lax.dynamic_index_in_dim(pair_sum, side, 0, keepdims=False)
        sent = lax.dynamic_index_in_dim(pair_sum, 1 - side, 0, keepdims=False)
        summed = kept.astype(jnp.float32) + lax.ppermute(
            sent, ROW[0], [(0, 1), (1, 0)]
        ).astype(jnp.float32)
        outputs.append((residual[low:high].astype(jnp.float32) + summed).astype(half_float))
    result = jnp.concatenate(outputs, axis=0)
    return (result[:rows_prompt], result[rows_prompt:])


def solution(mesh):
    col_size = mesh.shape["col"]
    fine_mesh = jax.sharding.Mesh(
        mesh.devices.reshape(mesh.shape["row"] // 2, 2, 4, col_size // 8, 2), ROW + COL
    )
    in_specs = (
        P(COL, ROW),
        P(COL, ROW),
        P(),
        P(),
        P(ROW + COL, None),
        P(ROW + COL, None),
        P(ROW + COL, None),
        P(ROW + COL, None),
        P(COL, ROW, None),
        P(COL, ROW, None),
        P(COL),
        P(),
        P(),
    )
    out_specs = (P(COL, ROW), P(COL, ROW))
    return jax.shard_map(
        on_device, mesh=fine_mesh, in_specs=in_specs, out_specs=out_specs, check_vma=False
    )
```

```python
import functools

import jax
import jax.numpy as jnp
from jax import lax
from jax.experimental import pallas as pl
from jax.experimental.pallas import tpu as pltpu
from jax.sharding import PartitionSpec as P

HD = 64
ROT = 32
PLEN = 512
CTX = 4096


NEG = -1e30
COL = ("col_y", "col_z", "col_x")
ROW = ("row_x", "row_core")


def layer_norm(rows, gain, bias):
    values = rows.astype(jnp.float32)
    centre = jnp.mean(values, axis=-1, keepdims=True)
    centred = values - centre
    deviation = jnp.mean(centred * centred, axis=-1, keepdims=True)
    return (centred * lax.rsqrt(deviation + 1e-05) * gain + bias).astype(jnp.bfloat16)


def rotary(vectors, position):
    half_width = ROT // 2
    frequency = 10000.0 ** (-2.0 * jnp.arange(half_width).astype(jnp.float32) / ROT)
    angle = position.astype(jnp.float32)[..., None, None] * frequency
    cosine = jnp.cos(angle)
    sine_value = jnp.sin(angle)
    lower_part = vectors[..., :half_width]
    upper_part = vectors[..., half_width:ROT]
    return jnp.concatenate(
        [
            lower_part * cosine - upper_part * sine_value,
            upper_part * cosine + lower_part * sine_value,
            vectors[..., ROT:],
        ],
        axis=-1,
    )


def attention_kernel(lengths_ref, query_ref, key_ref, value_ref, out_ref, *, heads):
    length = lengths_ref[pl.program_id(0)]
    rows = lax.broadcasted_iota(jnp.int32, (PLEN, PLEN), 0)
    cols = lax.broadcasted_iota(jnp.int32, (PLEN, PLEN), 1)
    allowed = (cols <= rows) & (cols < length)
    for head in range(heads):
        lanes = slice(head * HD, (head + 1) * HD)
        scores = lax.dot_general(
            query_ref[:, lanes], key_ref[:, lanes], (((1,), (1,)), ((), ())),
            preferred_element_type=jnp.float32,
        ) * (HD ** -0.5)
        scores = jnp.where(allowed, scores, NEG)
        top = jnp.max(scores, axis=-1, keepdims=True)
        raised = jnp.exp(scores - top)
        probs = (raised / jnp.sum(raised, axis=-1, keepdims=True)).astype(jnp.bfloat16)
        mixed = jnp.dot(probs, value_ref[:, lanes], preferred_element_type=jnp.float32)
        out_ref[:, lanes] = mixed.astype(jnp.bfloat16)


def prompt_attention(lengths, queries, keys, values, heads, interpret=False):
    rows, width = queries.shape
    block = pl.BlockSpec((PLEN, width), lambda p, lengths_ref: (p, 0))
    return pl.pallas_call(
        functools.partial(attention_kernel, heads=heads),
        out_shape=jax.ShapeDtypeStruct((rows, width), jnp.bfloat16),
        grid_spec=pltpu.PrefetchScalarGridSpec(
            num_scalar_prefetch=1,
            grid=(rows // PLEN,),
            in_specs=[block, block, block],
            out_specs=block,
        ),
        interpret=interpret,
    )(lengths, queries, keys, values)


def on_device(
    prompt_tokens,
    decode_tokens,
    norm_gain,
    norm_bias,
    project_weight,
    dense_weight,
    expand_weight,
    reduce_weight,
    key_cache,
    value_cache,
    prompt_lengths,
    cache_ages,
    slot_request,
):
    half_float = jnp.bfloat16
    row_count = lax.axis_size(ROW)
    col_count = lax.axis_size(COL)

    def by_row_group(weight):
        local_rows, width = weight.shape
        return weight.astype(half_float).reshape(local_rows, row_count, width // row_count)

    def regroup(weights):
        joined = jnp.concatenate([by_row_group(w) for w in weights], axis=2)
        me = lax.axis_index(ROW)
        received = [lax.dynamic_index_in_dim(joined, me, 1, keepdims=False)] + [
            lax.ppermute(
                lax.dynamic_index_in_dim(joined, (me + k) % row_count, 1, keepdims=False),
                ROW,
                [(j, (j + k) % row_count) for j in range(row_count)],
            )
            for k in range(1, row_count)
        ]
        by_source = jnp.stack(received, axis=0)
        flat = jnp.concatenate(
            [
                lax.dynamic_index_in_dim(by_source, (me - r) % row_count, 0, keepdims=False)
                for r in range(row_count)
            ],
            axis=0,
        )
        partner = lax.ppermute(flat, COL[-1], [(0, 1), (1, 0)])
        first = lax.axis_index(COL[-1]) == 0
        paired = jnp.concatenate(
            [jnp.where(first, flat, partner), jnp.where(first, partner, flat)], axis=0
        )
        gathered = lax.all_gather(paired, COL[:-1], axis=0, tiled=True)
        pieces = []
        offset = 0
        for w in weights:
            width = w.shape[1] // row_count
            pieces.append(gathered[:, offset:offset + width])
            offset += width
        return pieces

    def to_gathered(values):
        lead = values.shape[:-1]
        return (
            values.reshape(lead + (row_count, col_count, -1))
            .swapaxes(-3, -2)
            .reshape(lead + (-1,))
        )

    def from_gathered(values):
        lead = values.shape[:-1]
        return (
            values.reshape(lead + (col_count, row_count, -1))
            .swapaxes(-3, -2)
            .reshape(lead + (-1,))
        )

    w_project, w_dense = regroup((project_weight, dense_weight))
    w_expand, w_reduce = regroup((expand_weight, reduce_weight))
    local_joined = jnp.concatenate([prompt_tokens, decode_tokens], axis=0)
    row_index = lax.axis_index(ROW)
    shifted = [local_joined] + [
        lax.ppermute(
            local_joined, ROW, [(j, (j + k) % row_count) for j in range(row_count)]
        )
        for k in range(1, row_count)
    ]
    relative = jnp.stack(shifted, axis=0)
    blocks = jnp.stack(
        [
            lax.dynamic_index_in_dim(relative, (row_index - r) % row_count, 0, keepdims=False)
            for r in range(row_count)
        ],
        axis=0,
    )
    joined = (
        blocks.reshape(row_count, local_joined.shape[0], col_count, -1)
        .transpose(1, 2, 0, 3)
        .reshape(local_joined.shape[0], -1)
    )
    norm_gain = to_gathered(norm_gain)
    norm_bias = to_gathered(norm_bias)
    prompt_full = joined[: prompt_tokens.shape[0]]
    decode_full = joined[prompt_tokens.shape[0]:]
    rows_prompt = prompt_full.shape[0]
    slot_local = decode_full.shape[0]
    prompt_count = rows_prompt // PLEN
    heads_local = w_dense.shape[1] // HD
    total_slots = slot_request.shape[0]
    scale = HD ** (-0.5)
    normed = layer_norm(joined, norm_gain, norm_bias)
    merged = jnp.dot(normed, w_project, preferred_element_type=jnp.float32)
    prompt_pieces = merged[:rows_prompt].reshape(rows_prompt, heads_local, 3, HD)
    places = jnp.arange(rows_prompt, dtype=jnp.int32) % PLEN
    width = heads_local * HD
    prompt_queries = rotary(prompt_pieces[:, :, 0], places).astype(half_float).reshape(rows_prompt, width)
    prompt_keys = rotary(prompt_pieces[:, :, 1], places).astype(half_float).reshape(rows_prompt, width)
    prompt_values = prompt_pieces[:, :, 2].astype(half_float).reshape(rows_prompt, width)
    prompt_mixed = prompt_attention(
        prompt_lengths, prompt_queries, prompt_keys, prompt_values, heads_local
    )
    col_index = lax.axis_index(COL)
    first_slot = col_index * slot_local
    local_ids = first_slot + jnp.arange(slot_local, dtype=jnp.int32)
    own_request = lax.dynamic_slice_in_dim(slot_request, first_slot, slot_local)
    all_ids = jnp.arange(total_slots, dtype=jnp.int32)
    slot_match = own_request[:, None] == all_ids[None, :]
    slot_age = jnp.sum(jnp.where(slot_match, cache_ages[None, :], 0), axis=1)
    decode_pieces = merged[rows_prompt:].reshape(slot_local, heads_local, 3, HD)
    query_new = rotary(decode_pieces[:, :, 0], slot_age).astype(half_float)
    key_new = rotary(decode_pieces[:, :, 1], slot_age).astype(half_float)
    value_new = decode_pieces[:, :, 2].astype(half_float)
    packed = jnp.stack([query_new, key_new, value_new], axis=2).reshape(
        slot_local, heads_local * 3 * HD
    )
    handed = lax.all_to_all(
        jnp.broadcast_to(packed, (col_count,) + packed.shape[1:]),
        COL, split_axis=0, concat_axis=0, tiled=True,
    )
    chooser = (slot_request[None, :] == local_ids[:, None]).astype(half_float)
    mine = jnp.dot(chooser, handed, preferred_element_type=jnp.float32).astype(half_float)
    mine = mine.reshape(slot_local, heads_local, 3, HD)
    query = mine[:, :, 0]
    own_key = mine[:, :, 1]
    own_value = mine[:, :, 2]
    local_ages = lax.dynamic_slice_in_dim(cache_ages, first_slot, slot_local)
    keys_local = key_cache.reshape(slot_local, heads_local, CTX, HD)
    values_local = value_cache.reshape(slot_local, heads_local, CTX, HD)
    cache_scores = (
        jnp.einsum("shd,shtd->sht", query, keys_local, preferred_element_type=jnp.float32) * scale
    )
    key_places = jnp.arange(CTX, dtype=jnp.int32)
    cache_scores = jnp.where(
        key_places[None, None, :] < local_ages[:, None, None], cache_scores, NEG
    )
    own_score = jnp.sum(query.astype(jnp.float32) * own_key.astype(jnp.float32), axis=-1) * scale
    decode_top = jnp.maximum(jnp.max(cache_scores, axis=-1), own_score)
    cache_raised = jnp.exp(cache_scores - decode_top[:, :, None])
    own_raised = jnp.exp(own_score - decode_top)
    decode_total = jnp.sum(cache_raised, axis=-1) + own_raised
    cache_probs = (cache_raised / decode_total[:, :, None]).astype(half_float)
    own_prob = (own_raised / decode_total).astype(half_float)

    start_value = own_prob.astype(jnp.float32)[:, :, None] * own_value.astype(jnp.float32)
    decode_sum = start_value + jnp.einsum(
        "sht,shtd->shd", cache_probs, values_local, preferred_element_type=jnp.float32
    )
    decode_mixed = decode_sum.astype(half_float).reshape(slot_local, heads_local * HD)
    returned = lax.all_to_all(
        jnp.broadcast_to(decode_mixed, (col_count,) + decode_mixed.shape[1:]),
        COL, split_axis=0, concat_axis=0, tiled=True,
    )
    picker = slot_match.astype(half_float)
    decode_heads = jnp.dot(picker, returned, preferred_element_type=jnp.float32).astype(half_float)
    mixed_all = jnp.concatenate([prompt_mixed, decode_heads], axis=0)
    attn_part = lax.dot_general(
        mixed_all, w_dense, (((1,), (1,)), ((), ())), preferred_element_type=jnp.float32
    )
    residual = jnp.concatenate([prompt_tokens, decode_tokens], axis=0)
    bounds = [0, 3 * rows_prompt // 8, 3 * rows_prompt // 4, normed.shape[0]]
    outputs = []
    for low, high in zip(bounds[:-1], bounds[1:]):
        hidden = jax.nn.gelu(
            jnp.dot(normed[low:high], w_expand, preferred_element_type=jnp.float32),
            approximate=True,
        ).astype(half_float)
        mlp_part = lax.dot_general(
            hidden, w_reduce, (((1,), (1,)), ((), ())), preferred_element_type=jnp.float32
        )
        chunk = from_gathered(attn_part[low:high] + mlp_part).astype(half_float)
        chunk = chunk.reshape(high - low, 2, row_count // 2, -1).transpose(2, 1, 0, 3)
        core = lax.axis_index(ROW[1])
        mine = lax.dynamic_index_in_dim(chunk, core, 0, keepdims=False)
        other = lax.dynamic_index_in_dim(chunk, 1 - core, 0, keepdims=False)
        pair_sum = (
            mine.astype(jnp.float32)
            + lax.ppermute(other, ROW[1], [(0, 1), (1, 0)]).astype(jnp.float32)
        ).astype(half_float)
        side = lax.axis_index(ROW[0])
        kept = lax.dynamic_index_in_dim(pair_sum, side, 0, keepdims=False)
        sent = lax.dynamic_index_in_dim(pair_sum, 1 - side, 0, keepdims=False)
        summed = kept.astype(jnp.float32) + lax.ppermute(
            sent, ROW[0], [(0, 1), (1, 0)]
        ).astype(jnp.float32)
        outputs.append((residual[low:high].astype(jnp.float32) + summed).astype(half_float))
    result = jnp.concatenate(outputs, axis=0)
    return (result[:rows_prompt], result[rows_prompt:])


def solution(mesh):
    col_size = mesh.shape["col"]
    fine_mesh = jax.sharding.Mesh(
        mesh.devices.reshape(mesh.shape["row"] // 2, 2, 4, col_size // 8, 2), ROW + COL
    )
    in_specs = (
        P(COL, ROW),
        P(COL, ROW),
        P(),
        P(),
        P(ROW + COL, None),
        P(ROW + COL, None),
        P(ROW + COL, None),
        P(ROW + COL, None),
        P(COL, ROW, None),
        P(COL, ROW, None),
        P(COL),
        P(),
        P(),
    )
    out_specs = (P(COL, ROW), P(COL, ROW))
    return jax.shard_map(
        on_device, mesh=fine_mesh, in_specs=in_specs, out_specs=out_specs, check_vma=False
    )
```

```python
import functools

import jax
import jax.numpy as jnp
from jax import lax
from jax.experimental import pallas as pl
from jax.experimental.pallas import tpu as pltpu
from jax.sharding import PartitionSpec as P

HD = 64
ROT = 32
PLEN = 512
CTX = 4096


NEG = -1e30
COL = ("col_y", "col_z", "col_x")
ROW = ("row_x", "row_core")


def layer_norm(rows, gain, bias):
    values = rows.astype(jnp.float32)
    centre = jnp.mean(values, axis=-1, keepdims=True)
    centred = values - centre
    deviation = jnp.mean(centred * centred, axis=-1, keepdims=True)
    return (centred * lax.rsqrt(deviation + 1e-05) * gain + bias).astype(jnp.bfloat16)


def rotary(vectors, position):
    half_width = ROT // 2
    frequency = 10000.0 ** (-2.0 * jnp.arange(half_width).astype(jnp.float32) / ROT)
    angle = position.astype(jnp.float32)[..., None, None] * frequency
    cosine = jnp.cos(angle)
    sine_value = jnp.sin(angle)
    lower_part = vectors[..., :half_width]
    upper_part = vectors[..., half_width:ROT]
    return jnp.concatenate(
        [
            lower_part * cosine - upper_part * sine_value,
            upper_part * cosine + lower_part * sine_value,
            vectors[..., ROT:],
        ],
        axis=-1,
    )


def attention_kernel(lengths_ref, query_ref, key_ref, value_ref, out_ref, *, heads):
    length = lengths_ref[pl.program_id(0)]
    rows = lax.broadcasted_iota(jnp.int32, (PLEN, PLEN), 0)
    cols = lax.broadcasted_iota(jnp.int32, (PLEN, PLEN), 1)
    allowed = (cols <= rows) & (cols < length)
    for head in range(heads):
        lanes = slice(head * HD, (head + 1) * HD)
        scores = lax.dot_general(
            query_ref[:, lanes], key_ref[:, lanes], (((1,), (1,)), ((), ())),
            preferred_element_type=jnp.float32,
        ) * (HD ** -0.5)
        scores = jnp.where(allowed, scores, NEG)
        top = jnp.max(scores, axis=-1, keepdims=True)
        raised = jnp.exp(scores - top)
        probs = (raised / jnp.sum(raised, axis=-1, keepdims=True)).astype(jnp.bfloat16)
        mixed = jnp.dot(probs, value_ref[:, lanes], preferred_element_type=jnp.float32)
        out_ref[:, lanes] = mixed.astype(jnp.bfloat16)


def prompt_attention(lengths, queries, keys, values, heads, interpret=False):
    rows, width = queries.shape
    block = pl.BlockSpec((PLEN, width), lambda p, lengths_ref: (p, 0))
    return pl.pallas_call(
        functools.partial(attention_kernel, heads=heads),
        out_shape=jax.ShapeDtypeStruct((rows, width), jnp.bfloat16),
        grid_spec=pltpu.PrefetchScalarGridSpec(
            num_scalar_prefetch=1,
            grid=(rows // PLEN,),
            in_specs=[block, block, block],
            out_specs=block,
        ),
        interpret=interpret,
    )(lengths, queries, keys, values)


def on_device(
    prompt_tokens,
    decode_tokens,
    norm_gain,
    norm_bias,
    project_weight,
    dense_weight,
    expand_weight,
    reduce_weight,
    key_cache,
    value_cache,
    prompt_lengths,
    cache_ages,
    slot_request,
):
    half_float = jnp.bfloat16
    row_count = lax.axis_size(ROW)
    col_count = lax.axis_size(COL)

    def by_row_group(weight):
        local_rows, width = weight.shape
        return weight.astype(half_float).reshape(local_rows, row_count, width // row_count)

    def regroup(weights):
        joined = jnp.concatenate([by_row_group(w) for w in weights], axis=2)
        me = lax.axis_index(ROW)
        received = [lax.dynamic_index_in_dim(joined, me, 1, keepdims=False)] + [
            lax.ppermute(
                lax.dynamic_index_in_dim(joined, (me + k) % row_count, 1, keepdims=False),
                ROW,
                [(j, (j + k) % row_count) for j in range(row_count)],
            )
            for k in range(1, row_count)
        ]
        by_source = jnp.stack(received, axis=0)
        flat = jnp.concatenate(
            [
                lax.dynamic_index_in_dim(by_source, (me - r) % row_count, 0, keepdims=False)
                for r in range(row_count)
            ],
            axis=0,
        )
        partner = lax.ppermute(flat, COL[-1], [(0, 1), (1, 0)])
        first = lax.axis_index(COL[-1]) == 0
        paired = jnp.concatenate(
            [jnp.where(first, flat, partner), jnp.where(first, partner, flat)], axis=0
        )
        gathered = lax.all_gather(paired, COL[:-1], axis=0, tiled=True)
        pieces = []
        offset = 0
        for w in weights:
            width = w.shape[1] // row_count
            pieces.append(gathered[:, offset:offset + width])
            offset += width
        return pieces

    def to_gathered(values):
        lead = values.shape[:-1]
        return (
            values.reshape(lead + (row_count, col_count, -1))
            .swapaxes(-3, -2)
            .reshape(lead + (-1,))
        )

    def from_gathered(values):
        lead = values.shape[:-1]
        return (
            values.reshape(lead + (col_count, row_count, -1))
            .swapaxes(-3, -2)
            .reshape(lead + (-1,))
        )

    w_project, w_dense = regroup((project_weight, dense_weight))
    w_expand, w_reduce = regroup((expand_weight, reduce_weight))
    local_joined = jnp.concatenate([prompt_tokens, decode_tokens], axis=0)
    row_index = lax.axis_index(ROW)
    shifted = [local_joined] + [
        lax.ppermute(
            local_joined, ROW, [(j, (j + k) % row_count) for j in range(row_count)]
        )
        for k in range(1, row_count)
    ]
    relative = jnp.stack(shifted, axis=0)
    blocks = jnp.stack(
        [
            lax.dynamic_index_in_dim(relative, (row_index - r) % row_count, 0, keepdims=False)
            for r in range(row_count)
        ],
        axis=0,
    )
    joined = (
        blocks.reshape(row_count, local_joined.shape[0], col_count, -1)
        .transpose(1, 2, 0, 3)
        .reshape(local_joined.shape[0], -1)
    )
    norm_gain = to_gathered(norm_gain)
    norm_bias = to_gathered(norm_bias)
    prompt_full = joined[: prompt_tokens.shape[0]]
    decode_full = joined[prompt_tokens.shape[0]:]
    rows_prompt = prompt_full.shape[0]
    slot_local = decode_full.shape[0]
    prompt_count = rows_prompt // PLEN
    heads_local = w_dense.shape[1] // HD
    total_slots = slot_request.shape[0]
    scale = HD ** (-0.5)
    normed = layer_norm(joined, norm_gain, norm_bias)
    merged = jnp.dot(normed, w_project, preferred_element_type=jnp.float32)
    prompt_pieces = merged[:rows_prompt].reshape(rows_prompt, heads_local, 3, HD)
    places = jnp.arange(rows_prompt, dtype=jnp.int32) % PLEN
    width = heads_local * HD
    prompt_queries = rotary(prompt_pieces[:, :, 0], places).astype(half_float).reshape(rows_prompt, width)
    prompt_keys = rotary(prompt_pieces[:, :, 1], places).astype(half_float).reshape(rows_prompt, width)
    prompt_values = prompt_pieces[:, :, 2].astype(half_float).reshape(rows_prompt, width)
    prompt_mixed = prompt_attention(
        prompt_lengths, prompt_queries, prompt_keys, prompt_values, heads_local
    )
    col_index = lax.axis_index(COL)
    first_slot = col_index * slot_local
    local_ids = first_slot + jnp.arange(slot_local, dtype=jnp.int32)
    own_request = lax.dynamic_slice_in_dim(slot_request, first_slot, slot_local)
    all_ids = jnp.arange(total_slots, dtype=jnp.int32)
    slot_match = own_request[:, None] == all_ids[None, :]
    slot_age = jnp.sum(jnp.where(slot_match, cache_ages[None, :], 0), axis=1)
    decode_pieces = merged[rows_prompt:].reshape(slot_local, heads_local, 3, HD)
    query_new = rotary(decode_pieces[:, :, 0], slot_age).astype(half_float)
    key_new = rotary(decode_pieces[:, :, 1], slot_age).astype(half_float)
    value_new = decode_pieces[:, :, 2].astype(half_float)
    packed = jnp.stack([query_new, key_new, value_new], axis=2).reshape(
        slot_local, heads_local * 3 * HD
    )
    handed = lax.all_to_all(
        jnp.broadcast_to(packed, (col_count,) + packed.shape[1:]),
        COL, split_axis=0, concat_axis=0, tiled=True,
    )
    chooser = (slot_request[None, :] == local_ids[:, None]).astype(half_float)
    mine = jnp.dot(chooser, handed, preferred_element_type=jnp.float32).astype(half_float)
    mine = mine.reshape(slot_local, heads_local, 3, HD)
    query = mine[:, :, 0]
    own_key = mine[:, :, 1]
    own_value = mine[:, :, 2]
    local_ages = lax.dynamic_slice_in_dim(cache_ages, first_slot, slot_local)
    keys_local = key_cache.reshape(slot_local, heads_local, CTX, HD)
    values_local = value_cache.reshape(slot_local, heads_local, CTX, HD)
    cache_scores = (
        jnp.einsum("shd,shtd->sht", query, keys_local, preferred_element_type=jnp.float32) * scale
    )
    key_places = jnp.arange(CTX, dtype=jnp.int32)
    cache_scores = jnp.where(
        key_places[None, None, :] < local_ages[:, None, None], cache_scores, NEG
    )
    own_score = jnp.sum(query.astype(jnp.float32) * own_key.astype(jnp.float32), axis=-1) * scale
    decode_top = jnp.maximum(jnp.max(cache_scores, axis=-1), own_score)
    cache_raised = jnp.exp(cache_scores - decode_top[:, :, None])
    own_raised = jnp.exp(own_score - decode_top)
    decode_total = jnp.sum(cache_raised, axis=-1) + own_raised
    cache_probs = (cache_raised / decode_total[:, :, None]).astype(half_float)
    own_prob = (own_raised / decode_total).astype(half_float)

    start_value = own_prob.astype(jnp.float32)[:, :, None] * own_value.astype(jnp.float32)
    decode_sum = start_value + jnp.einsum(
        "sht,shtd->shd", cache_probs, values_local, preferred_element_type=jnp.float32
    )
    decode_mixed = decode_sum.astype(half_float).reshape(slot_local, heads_local * HD)
    returned = lax.all_to_all(
        jnp.broadcast_to(decode_mixed, (col_count,) + decode_mixed.shape[1:]),
        COL, split_axis=0, concat_axis=0, tiled=True,
    )
    picker = slot_match.astype(half_float)
    decode_heads = jnp.dot(picker, returned, preferred_element_type=jnp.float32).astype(half_float)
    mixed_all = jnp.concatenate([prompt_mixed, decode_heads], axis=0)
    attn_part = lax.dot_general(
        mixed_all, w_dense, (((1,), (1,)), ((), ())), preferred_element_type=jnp.float32
    )
    residual = jnp.concatenate([prompt_tokens, decode_tokens], axis=0)
    bounds = [0, 5 * rows_prompt // 8, normed.shape[0]]
    outputs = []
    for low, high in zip(bounds[:-1], bounds[1:]):
        hidden = jax.nn.gelu(
            jnp.dot(normed[low:high], w_expand, preferred_element_type=jnp.float32),
            approximate=True,
        ).astype(half_float)
        mlp_part = lax.dot_general(
            hidden, w_reduce, (((1,), (1,)), ((), ())), preferred_element_type=jnp.float32
        )
        chunk = from_gathered(attn_part[low:high] + mlp_part).astype(half_float)
        chunk = chunk.reshape(high - low, 2, row_count // 2, -1).transpose(2, 1, 0, 3)
        core = lax.axis_index(ROW[1])
        mine = lax.dynamic_index_in_dim(chunk, core, 0, keepdims=False)
        other = lax.dynamic_index_in_dim(chunk, 1 - core, 0, keepdims=False)
        pair_sum = (
            mine.astype(jnp.float32)
            + lax.ppermute(other, ROW[1], [(0, 1), (1, 0)]).astype(jnp.float32)
        ).astype(half_float)
        side = lax.axis_index(ROW[0])
        kept = lax.dynamic_index_in_dim(pair_sum, side, 0, keepdims=False)
        sent = lax.dynamic_index_in_dim(pair_sum, 1 - side, 0, keepdims=False)
        summed = kept.astype(jnp.float32) + lax.ppermute(
            sent, ROW[0], [(0, 1), (1, 0)]
        ).astype(jnp.float32)
        outputs.append((residual[low:high].astype(jnp.float32) + summed).astype(half_float))
    result = jnp.concatenate(outputs, axis=0)
    return (result[:rows_prompt], result[rows_prompt:])


def solution(mesh):
    col_size = mesh.shape["col"]
    fine_mesh = jax.sharding.Mesh(
        mesh.devices.reshape(mesh.shape["row"] // 2, 2, 4, col_size // 8, 2), ROW + COL
    )
    in_specs = (
        P(COL, ROW),
        P(COL, ROW),
        P(),
        P(),
        P(ROW + COL, None),
        P(ROW + COL, None),
        P(ROW + COL, None),
        P(ROW + COL, None),
        P(COL, ROW, None),
        P(COL, ROW, None),
        P(COL),
        P(),
        P(),
    )
    out_specs = (P(COL, ROW), P(COL, ROW))
    return jax.shard_map(
        on_device, mesh=fine_mesh, in_specs=in_specs, out_specs=out_specs, check_vma=False
    )
```

```python
import functools

import jax
import jax.numpy as jnp
from jax import lax
from jax.experimental import pallas as pl
from jax.experimental.pallas import tpu as pltpu
from jax.sharding import PartitionSpec as P

HD = 64
ROT = 32
PLEN = 512
CTX = 4096


NEG = -1e30
COL = ("col_y", "col_z", "col_x")
ROW = ("row_x", "row_core")


def layer_norm(rows, gain, bias):
    values = rows.astype(jnp.float32)
    centre = jnp.mean(values, axis=-1, keepdims=True)
    centred = values - centre
    deviation = jnp.mean(centred * centred, axis=-1, keepdims=True)
    return (centred * lax.rsqrt(deviation + 1e-05) * gain + bias).astype(jnp.bfloat16)


def rotary(vectors, position):
    half_width = ROT // 2
    frequency = 10000.0 ** (-2.0 * jnp.arange(half_width).astype(jnp.float32) / ROT)
    angle = position.astype(jnp.float32)[..., None, None] * frequency
    cosine = jnp.cos(angle)
    sine_value = jnp.sin(angle)
    lower_part = vectors[..., :half_width]
    upper_part = vectors[..., half_width:ROT]
    return jnp.concatenate(
        [
            lower_part * cosine - upper_part * sine_value,
            upper_part * cosine + lower_part * sine_value,
            vectors[..., ROT:],
        ],
        axis=-1,
    )


def attention_kernel(lengths_ref, query_ref, key_ref, value_ref, out_ref, *, heads):
    length = lengths_ref[pl.program_id(0)]
    rows = lax.broadcasted_iota(jnp.int32, (PLEN, PLEN), 0)
    cols = lax.broadcasted_iota(jnp.int32, (PLEN, PLEN), 1)
    allowed = (cols <= rows) & (cols < length)
    for head in range(heads):
        lanes = slice(head * HD, (head + 1) * HD)
        scores = lax.dot_general(
            query_ref[:, lanes], key_ref[:, lanes], (((1,), (1,)), ((), ())),
            preferred_element_type=jnp.float32,
        ) * (HD ** -0.5)
        scores = jnp.where(allowed, scores, NEG)
        top = jnp.max(scores, axis=-1, keepdims=True)
        raised = jnp.exp(scores - top)
        probs = (raised / jnp.sum(raised, axis=-1, keepdims=True)).astype(jnp.bfloat16)
        mixed = jnp.dot(probs, value_ref[:, lanes], preferred_element_type=jnp.float32)
        out_ref[:, lanes] = mixed.astype(jnp.bfloat16)


def prompt_attention(lengths, queries, keys, values, heads, interpret=False):
    rows, width = queries.shape
    block = pl.BlockSpec((PLEN, width), lambda p, lengths_ref: (p, 0))
    return pl.pallas_call(
        functools.partial(attention_kernel, heads=heads),
        out_shape=jax.ShapeDtypeStruct((rows, width), jnp.bfloat16),
        grid_spec=pltpu.PrefetchScalarGridSpec(
            num_scalar_prefetch=1,
            grid=(rows // PLEN,),
            in_specs=[block, block, block],
            out_specs=block,
        ),
        interpret=interpret,
    )(lengths, queries, keys, values)


def on_device(
    prompt_tokens,
    decode_tokens,
    norm_gain,
    norm_bias,
    project_weight,
    dense_weight,
    expand_weight,
    reduce_weight,
    key_cache,
    value_cache,
    prompt_lengths,
    cache_ages,
    slot_request,
):
    half_float = jnp.bfloat16
    row_count = lax.axis_size(ROW)
    col_count = lax.axis_size(COL)

    def by_row_group(weight):
        local_rows, width = weight.shape
        return weight.astype(half_float).reshape(local_rows, row_count, width // row_count)

    def regroup(weights):
        joined = jnp.concatenate([by_row_group(w) for w in weights], axis=2)
        me = lax.axis_index(ROW)
        received = [lax.dynamic_index_in_dim(joined, me, 1, keepdims=False)] + [
            lax.ppermute(
                lax.dynamic_index_in_dim(joined, (me + k) % row_count, 1, keepdims=False),
                ROW,
                [(j, (j + k) % row_count) for j in range(row_count)],
            )
            for k in range(1, row_count)
        ]
        by_source = jnp.stack(received, axis=0)
        flat = jnp.concatenate(
            [
                lax.dynamic_index_in_dim(by_source, (me - r) % row_count, 0, keepdims=False)
                for r in range(row_count)
            ],
            axis=0,
        )
        partner = lax.ppermute(flat, COL[-1], [(0, 1), (1, 0)])
        first = lax.axis_index(COL[-1]) == 0
        paired = jnp.concatenate(
            [jnp.where(first, flat, partner), jnp.where(first, partner, flat)], axis=0
        )
        gathered = lax.all_gather(paired, COL[:-1], axis=0, tiled=True)
        pieces = []
        offset = 0
        for w in weights:
            width = w.shape[1] // row_count
            pieces.append(gathered[:, offset:offset + width])
            offset += width
        return pieces

    def to_gathered(values):
        lead = values.shape[:-1]
        return (
            values.reshape(lead + (row_count, col_count, -1))
            .swapaxes(-3, -2)
            .reshape(lead + (-1,))
        )

    def from_gathered(values):
        lead = values.shape[:-1]
        return (
            values.reshape(lead + (col_count, row_count, -1))
            .swapaxes(-3, -2)
            .reshape(lead + (-1,))
        )

    w_project, w_dense = regroup((project_weight, dense_weight))
    w_expand, w_reduce = regroup((expand_weight, reduce_weight))
    local_joined = jnp.concatenate([prompt_tokens, decode_tokens], axis=0)
    row_index = lax.axis_index(ROW)
    shifted = [local_joined] + [
        lax.ppermute(
            local_joined, ROW, [(j, (j + k) % row_count) for j in range(row_count)]
        )
        for k in range(1, row_count)
    ]
    relative = jnp.stack(shifted, axis=0)
    blocks = jnp.stack(
        [
            lax.dynamic_index_in_dim(relative, (row_index - r) % row_count, 0, keepdims=False)
            for r in range(row_count)
        ],
        axis=0,
    )
    joined = (
        blocks.reshape(row_count, local_joined.shape[0], col_count, -1)
        .transpose(1, 2, 0, 3)
        .reshape(local_joined.shape[0], -1)
    )
    norm_gain = to_gathered(norm_gain)
    norm_bias = to_gathered(norm_bias)
    prompt_full = joined[: prompt_tokens.shape[0]]
    decode_full = joined[prompt_tokens.shape[0]:]
    rows_prompt = prompt_full.shape[0]
    slot_local = decode_full.shape[0]
    prompt_count = rows_prompt // PLEN
    heads_local = w_dense.shape[1] // HD
    total_slots = slot_request.shape[0]
    scale = HD ** (-0.5)
    normed = layer_norm(joined, norm_gain, norm_bias)
    merged = jnp.dot(normed, w_project, preferred_element_type=jnp.float32)
    prompt_pieces = merged[:rows_prompt].reshape(rows_prompt, heads_local, 3, HD)
    places = jnp.arange(rows_prompt, dtype=jnp.int32) % PLEN
    width = heads_local * HD
    prompt_queries = rotary(prompt_pieces[:, :, 0], places).astype(half_float).reshape(rows_prompt, width)
    prompt_keys = rotary(prompt_pieces[:, :, 1], places).astype(half_float).reshape(rows_prompt, width)
    prompt_values = prompt_pieces[:, :, 2].astype(half_float).reshape(rows_prompt, width)
    prompt_mixed = prompt_attention(
        prompt_lengths, prompt_queries, prompt_keys, prompt_values, heads_local
    )
    col_index = lax.axis_index(COL)
    first_slot = col_index * slot_local
    local_ids = first_slot + jnp.arange(slot_local, dtype=jnp.int32)
    own_request = lax.dynamic_slice_in_dim(slot_request, first_slot, slot_local)
    all_ids = jnp.arange(total_slots, dtype=jnp.int32)
    slot_match = own_request[:, None] == all_ids[None, :]
    slot_age = jnp.sum(jnp.where(slot_match, cache_ages[None, :], 0), axis=1)
    decode_pieces = merged[rows_prompt:].reshape(slot_local, heads_local, 3, HD)
    query_new = rotary(decode_pieces[:, :, 0], slot_age).astype(half_float)
    key_new = rotary(decode_pieces[:, :, 1], slot_age).astype(half_float)
    value_new = decode_pieces[:, :, 2].astype(half_float)
    packed = jnp.stack([query_new, key_new, value_new], axis=2).reshape(
        slot_local, heads_local * 3 * HD
    )
    handed = lax.all_to_all(
        jnp.broadcast_to(packed, (col_count,) + packed.shape[1:]),
        COL, split_axis=0, concat_axis=0, tiled=True,
    )
    chooser = (slot_request[None, :] == local_ids[:, None]).astype(half_float)
    mine = jnp.dot(chooser, handed, preferred_element_type=jnp.float32).astype(half_float)
    mine = mine.reshape(slot_local, heads_local, 3, HD)
    query = mine[:, :, 0]
    own_key = mine[:, :, 1]
    own_value = mine[:, :, 2]
    local_ages = lax.dynamic_slice_in_dim(cache_ages, first_slot, slot_local)
    keys_local = key_cache.reshape(slot_local, heads_local, CTX, HD)
    values_local = value_cache.reshape(slot_local, heads_local, CTX, HD)
    cache_scores = (
        jnp.einsum("shd,shtd->sht", query, keys_local, preferred_element_type=jnp.float32) * scale
    )
    key_places = jnp.arange(CTX, dtype=jnp.int32)
    cache_scores = jnp.where(
        key_places[None, None, :] < local_ages[:, None, None], cache_scores, NEG
    )
    own_score = jnp.sum(query.astype(jnp.float32) * own_key.astype(jnp.float32), axis=-1) * scale
    decode_top = jnp.maximum(jnp.max(cache_scores, axis=-1), own_score)
    cache_raised = jnp.exp(cache_scores - decode_top[:, :, None])
    own_raised = jnp.exp(own_score - decode_top)
    decode_total = jnp.sum(cache_raised, axis=-1) + own_raised
    cache_probs = (cache_raised / decode_total[:, :, None]).astype(half_float)
    own_prob = (own_raised / decode_total).astype(half_float)

    start_value = own_prob.astype(jnp.float32)[:, :, None] * own_value.astype(jnp.float32)
    decode_sum = start_value + jnp.einsum(
        "sht,shtd->shd", cache_probs, values_local, preferred_element_type=jnp.float32
    )
    decode_mixed = decode_sum.astype(half_float).reshape(slot_local, heads_local * HD)
    returned = lax.all_to_all(
        jnp.broadcast_to(decode_mixed, (col_count,) + decode_mixed.shape[1:]),
        COL, split_axis=0, concat_axis=0, tiled=True,
    )
    picker = slot_match.astype(half_float)
    decode_heads = jnp.dot(picker, returned, preferred_element_type=jnp.float32).astype(half_float)
    mixed_all = jnp.concatenate([prompt_mixed, decode_heads], axis=0)
    attn_part = lax.dot_general(
        mixed_all, w_dense, (((1,), (1,)), ((), ())), preferred_element_type=jnp.float32
    )
    residual = jnp.concatenate([prompt_tokens, decode_tokens], axis=0)
    bounds = [0, rows_prompt // 2, normed.shape[0]]
    outputs = []
    for low, high in zip(bounds[:-1], bounds[1:]):
        hidden = jax.nn.gelu(
            jnp.dot(normed[low:high], w_expand, preferred_element_type=jnp.float32),
            approximate=True,
        ).astype(half_float)
        mlp_part = lax.dot_general(
            hidden, w_reduce, (((1,), (1,)), ((), ())), preferred_element_type=jnp.float32
        )
        chunk = from_gathered(attn_part[low:high] + mlp_part).astype(half_float)
        chunk = chunk.reshape(high - low, 2, row_count // 2, -1).transpose(2, 1, 0, 3)
        core = lax.axis_index(ROW[1])
        mine = lax.dynamic_index_in_dim(chunk, core, 0, keepdims=False)
        other = lax.dynamic_index_in_dim(chunk, 1 - core, 0, keepdims=False)
        pair_sum = (
            mine.astype(jnp.float32)
            + lax.ppermute(other, ROW[1], [(0, 1), (1, 0)]).astype(jnp.float32)
        ).astype(half_float)
        side = lax.axis_index(ROW[0])
        kept = lax.dynamic_index_in_dim(pair_sum, side, 0, keepdims=False)
        sent = lax.dynamic_index_in_dim(pair_sum, 1 - side, 0, keepdims=False)
        summed = kept.astype(jnp.float32) + lax.ppermute(
            sent, ROW[0], [(0, 1), (1, 0)]
        ).astype(jnp.float32)
        outputs.append((residual[low:high].astype(jnp.float32) + summed).astype(half_float))
    last_prompt = rows_prompt - bounds[-2]
    prompt_result = jnp.concatenate(outputs[:-1] + [outputs[-1][:last_prompt]], axis=0)
    return (prompt_result, outputs[-1][last_prompt:])


def solution(mesh):
    col_size = mesh.shape["col"]
    fine_mesh = jax.sharding.Mesh(
        mesh.devices.reshape(mesh.shape["row"] // 2, 2, 4, col_size // 8, 2), ROW + COL
    )
    in_specs = (
        P(COL, ROW),
        P(COL, ROW),
        P(),
        P(),
        P(ROW + COL, None),
        P(ROW + COL, None),
        P(ROW + COL, None),
        P(ROW + COL, None),
        P(COL, ROW, None),
        P(COL, ROW, None),
        P(COL),
        P(),
        P(),
    )
    out_specs = (P(COL, ROW), P(COL, ROW))
    return jax.shard_map(
        on_device, mesh=fine_mesh, in_specs=in_specs, out_specs=out_specs, check_vma=False
    )
```
